32 devices in a mesh: prop: 2 (over x), tx: 4 (over y, core), ty: 4 (over z).
Axes of the slice: x: 2, y: 2, z: 4, core: 2. Of those that a mesh axis runs over, the one named last changes fastest.
Arguments:
- electric: float32 [3, 8, 32, 512], P(None, 'prop', 'ty', 'tx'), may hold values from -6 to 6
- magnetic: float32 [3, 8, 32, 512], P(None, 'prop', 'ty', 'tx'), may hold values from -6 to 6
- polarization: float32 [2, 3, 8, 32, 512], P(None, None, 'prop', 'ty', 'tx'), may hold values from -4 to 4
- current: float32 [2, 3, 8, 32, 512], P(None, None, 'prop', 'ty', 'tx'), may hold values from -4 to 4
- material: int32 [32, 512], P('ty', 'tx'), may hold values from 0 to 7
- advance: int32 [4], replicated, may hold values from 0 to 2, as said below
- permittivity: float32 [8], replicated, may hold values from 1.5 to 6
- nonlinear: float32 [8], replicated, may hold values from 0.05 to 0.5
- pole_strength: float32 [2, 8], replicated, may hold values from 0.3 to 3
- pole_frequency: float32 [2, 8], replicated, may hold values from 0.3 to 1.5
- pole_damping: float32 [2, 8], replicated, may hold values from 0.05 to 1
Outputs:
- electric_out: float32 [3, 8, 32, 512], P(None, 'prop', 'ty', 'tx')
- magnetic_out: float32 [3, 8, 32, 512], P(None, 'prop', 'ty', 'tx')
- polarization_out: float32 [2, 3, 8, 32, 512], P(None, None, 'prop', 'ty', 'tx')
- current_out: float32 [2, 3, 8, 32, 512], P(None, None, 'prop', 'ty', 'tx')
- column_energy: float32 [8, 32, 512], P('prop', 'ty', 'tx')
The draws below stay inside these ranges and needn't reach their ends.
Inputs may be any that keep to these rules, and one draw needn't show every extreme that they name: `advance`: at least one of the 4 entries equals 2.
All inputs are finite; a program needn't handle non-finite values.
Results may differ from the reference program's by a relative error of at most 0.0001.
Values sent between devices are 32-bit elements; how exact they have to be, the bound alone decides.
No kernel may reach another device: no remote copies, remote signals or barrier semaphores. Data moves between devices by JAX's collectives and lax.ppermute only.
A program may use at most 64 MiB of HBM per device.

```python
import math
import jax
import jax.numpy as jnp
from jax import lax

STEPS = 4
WSHIFT = 2
MATS = 8
NZ = 8
NY = 32
NX = 512


def draw_advance(key, part):
    counts = jax.random.randint(key, (STEPS,), 0, WSHIFT + 1)
    chosen = jax.random.randint(jax.random.fold_in(key, 7), (), 0, STEPS)
    return counts.at[chosen].set(WSHIFT).astype(jnp.int32)


def place_ends(array, stream_key, least, high):
    dims = array.shape
    spot = [jax.random.randint(jax.random.fold_in(stream_key, axis), (), 0, dims[axis]) for axis in range(len(dims))]
    array = array.at[tuple(spot)].set(least)
    longest = dims.index(max(dims))
    spot[longest] = (spot[longest] + 1) % dims[longest]
    return array.at[tuple(spot)].set(high)


def block_levels(stream_key, extent, split, smallest, largest):
    def one(dim, parts):
        steps = jax.random.uniform(jax.random.fold_in(jax.random.fold_in(stream_key, 6), dim), (parts,), jnp.float32, smallest / len(split), largest / len(split))
        return jnp.repeat(jnp.exp(steps), extent[dim] // parts).reshape((-1,) + (1,) * (len(extent) - dim - 1))

    loudness = one(*split[0])
    for cut in split[1:]:
        loudness = loudness * one(*cut)
    return loudness


def gaussian(own_key, shape, scale, bound, shards=(), kind=jnp.bfloat16):
    values = jax.random.normal(own_key, shape, jnp.float32) * scale
    if len(shards) > 0:
        values = block_levels(own_key, shape, shards, -0.22, 0.18) * values
    return jnp.clip(values, min=-bound, max=bound).astype(kind)


def setup_inputs(seed: int = 0) -> dict:
    splits = jax.random.split(jax.random.key(seed), 12)
    electric = gaussian(splits[0], (3, NZ, NY, NX), 1.0, 6.0, ((1, 2), (2, 4), (3, 4)), jnp.float32)
    magnetic = gaussian(splits[1], (3, NZ, NY, NX), 1.0, 6.0, ((1, 2), (2, 4), (3, 4)), jnp.float32)
    polarization = gaussian(splits[2], (2, 3, NZ, NY, NX), 0.5, 4.0, ((2, 2), (3, 4), (4, 4)), jnp.float32)
    current = gaussian(splits[3], (2, 3, NZ, NY, NX), 0.5, 4.0, ((2, 2), (3, 4), (4, 4)), jnp.float32)
    material = place_ends(jax.random.randint(splits[4], (NY, NX), 0, MATS), jax.random.fold_in(splits[4], 1), 0, MATS - 1).astype(jnp.int32)
    advance = draw_advance(jax.random.fold_in(splits[11], 71), 0)
    permittivity = jnp.clip(jnp.exp(jax.random.uniform(splits[6], (MATS,), jnp.float32, math.log(1.5), math.log(6.0))), 1.5, 6.0)
    nonlinear = jnp.clip(jnp.exp(jax.random.uniform(splits[7], (MATS,), jnp.float32, math.log(0.05), math.log(0.5))), 0.05, 0.5)
    pole_strength = jnp.clip(jnp.exp(jax.random.uniform(splits[8], (2, MATS), jnp.float32, math.log(0.3), math.log(3.0))), 0.3, 3.0)
    pole_frequency = jnp.clip(jnp.exp(jax.random.uniform(splits[9], (2, MATS), jnp.float32, math.log(0.3), math.log(1.5))), 0.3, 1.5)
    pole_damping = jnp.clip(jnp.exp(jax.random.uniform(splits[10], (2, MATS), jnp.float32, math.log(0.05), math.log(1.0))), 0.05, 1.0)
    return {"electric": electric, "magnetic": magnetic, "polarization": polarization, "current": current, "material": material, "advance": advance, "permittivity": permittivity, "nonlinear": nonlinear, "pole_strength": pole_strength, "pole_frequency": pole_frequency, "pole_damping": pole_damping}


time_step = 0.5


def upper_next(values, dimension):
    zeros_plane = jnp.zeros_like(lax.slice_in_dim(values, 0, 1, axis=dimension))
    rest = lax.slice_in_dim(values, 1, values.shape[dimension], axis=dimension)
    return jnp.concatenate([rest, zeros_plane], axis=dimension)


def lower_next(values, dimension):
    zeros_plane = jnp.zeros_like(lax.slice_in_dim(values, 0, 1, axis=dimension))
    rest = lax.slice_in_dim(values, 0, values.shape[dimension] - 1, axis=dimension)
    return jnp.concatenate([zeros_plane, rest], axis=dimension)


def forward_diff(values, dimension):
    return upper_next(values, dimension) - values


def backward_diff(values, dimension):
    return values - lower_next(values, dimension)


def curl_forward(field):
    field_x, field_y, field_z = field[0], field[1], field[2]
    return jnp.stack([forward_diff(field_z, 1) - forward_diff(field_y, 0),
                      forward_diff(field_x, 0) - forward_diff(field_z, 2),
                      forward_diff(field_y, 2) - forward_diff(field_x, 1)])


def curl_backward(field):
    field_x, field_y, field_z = field[0], field[1], field[2]
    return jnp.stack([backward_diff(field_z, 1) - backward_diff(field_y, 0),
                      backward_diff(field_x, 0) - backward_diff(field_z, 2),
                      backward_diff(field_y, 2) - backward_diff(field_x, 1)])


def advance_planes(values, amount, dimension):
    shape_pad = list(values.shape)
    shape_pad[dimension] = WSHIFT
    joined = jnp.concatenate([values, jnp.zeros(shape_pad, jnp.float32)], axis=dimension)
    return lax.dynamic_slice_in_dim(joined, amount, values.shape[dimension], axis=dimension)


def reference(electric, magnetic, polarization, current, material, advance, permittivity, nonlinear, pole_strength, pole_frequency, pole_damping):
    eps_cell = permittivity[material]
    kerr_cell = nonlinear[material]
    strength = pole_strength[:, material][:, None, None]
    frequency = pole_frequency[:, material]
    half_damp = 0.5 * time_step * pole_damping[:, material]
    keep_rate = ((1.0 - half_damp) / (1.0 + half_damp))[:, None, None]
    drive_rate = (time_step * frequency * frequency / (1.0 + half_damp))[:, None, None]
    for moment in range(STEPS):
        magnetic = magnetic - time_step * curl_forward(electric)
        squared = jnp.sum(electric * electric, axis=0)
        current = keep_rate * current + drive_rate * (strength * electric[None] - polarization)
        polarization = polarization + time_step * current
        electric = electric + time_step * (curl_backward(magnetic) - current[0] - current[1]) / (eps_cell + kerr_cell * squared)
        amount = advance[moment].astype(jnp.int32)
        electric = advance_planes(electric, amount, 1)
        magnetic = advance_planes(magnetic, amount, 1)
        polarization = advance_planes(polarization, amount, 2)
        current = advance_planes(current, amount, 2)
    density = eps_cell * jnp.sum(electric * electric, axis=0) + jnp.sum(magnetic * magnetic, axis=0)
    column_energy = jnp.cumsum(density, axis=0) / jnp.float32(NZ)
    return electric, magnetic, polarization, current, column_energy
```

```python
import jax
import jax.numpy as jnp
from jax import lax
from jax.sharding import PartitionSpec as P

STEPS = 4
WSHIFT = 2


time_step = 0.5


def from_offsets(value, axis, offsets):
    count, mine = (lax.axis_size(axis), lax.axis_index(axis))
    got = {}
    for k in offsets:
        if k in got:
            continue
        pairs = [(s, s - k) for s in range(count) if 0 <= s - k < count]
        if not pairs:
            got[k] = jnp.zeros_like(value)
            continue
        if -k in offsets and 2 * abs(k) >= count:
            pairs = pairs + [(s, s + k) for s in range(count) if 0 <= s + k < count]
            received = lax.ppermute(value, axis, pairs)
            for j in (k, -k):
                inside = jnp.logical_and(mine + j >= 0, mine + j < count)
                got[j] = jnp.where(inside, received, jnp.zeros_like(received))
            continue
        got[k] = lax.ppermute(value, axis, pairs)
    return got


def with_halo(cells, axis, dim, width):
    length = cells.shape[dim]
    head = lax.slice_in_dim(cells, 0, width, axis=dim)
    tail = lax.slice_in_dim(cells, length - width, length, axis=dim)
    below = from_offsets(tail, axis, (-1,))[-1]
    above = from_offsets(head, axis, (1,))[1]
    return jnp.concatenate([below, cells, above], axis=dim)


def upper_next(values, dimension):
    zeros_plane = jnp.zeros_like(lax.slice_in_dim(values, 0, 1, axis=dimension))
    rest = lax.slice_in_dim(values, 1, values.shape[dimension], axis=dimension)
    return jnp.concatenate([rest, zeros_plane], axis=dimension)


def lower_next(values, dimension):
    zeros_plane = jnp.zeros_like(lax.slice_in_dim(values, 0, 1, axis=dimension))
    rest = lax.slice_in_dim(values, 0, values.shape[dimension] - 1, axis=dimension)
    return jnp.concatenate([zeros_plane, rest], axis=dimension)


def forward_diff(values, dimension):
    return upper_next(values, dimension) - values


def backward_diff(values, dimension):
    return values - lower_next(values, dimension)


def curl_forward(field):
    field_x, field_y, field_z = field[0], field[1], field[2]
    return jnp.stack([forward_diff(field_z, 1) - forward_diff(field_y, 0),
                      forward_diff(field_x, 0) - forward_diff(field_z, 2),
                      forward_diff(field_y, 2) - forward_diff(field_x, 1)])


def curl_backward(field):
    field_x, field_y, field_z = field[0], field[1], field[2]
    return jnp.stack([backward_diff(field_z, 1) - backward_diff(field_y, 0),
                      backward_diff(field_x, 0) - backward_diff(field_z, 2),
                      backward_diff(field_y, 2) - backward_diff(field_x, 1)])


def advance_planes(values, amount, dimension):
    shape_pad = list(values.shape)
    shape_pad[dimension] = WSHIFT
    joined = jnp.concatenate([values, jnp.zeros(shape_pad, values.dtype)], axis=dimension)
    return lax.dynamic_slice_in_dim(joined, amount, values.shape[dimension], axis=dimension)


def cell_lookup(selector, table):
    return jnp.sum(jnp.where(selector, table[:, None, None], jnp.float32(0.0)), axis=0)


def inside_range(start, length, total, dimension, total_dims):
    shape_one = [1] * total_dims
    shape_one[dimension] = length
    marks = start + lax.broadcasted_iota(jnp.int32, tuple(shape_one), dimension)
    return jnp.logical_and(marks >= 0, marks < total)


def entering(value, axis):
    count, mine = (lax.axis_size(axis), lax.axis_index(axis))
    pieces = lax.all_gather(value, axis)
    running = jnp.zeros_like(value)
    for position in range(count - 1):
        running = jnp.where(position < mine, running + pieces[position], running)
    return running


def body(
    electric,
    magnetic,
    polarization,
    current,
    material,
    advance,
    permittivity,
    nonlinear,
    pole_strength,
    pole_frequency,
    pole_damping,
):
    planes, rows, columns = (electric.shape[1], electric.shape[2], electric.shape[3])
    n_prop, n_tx, n_ty = (lax.axis_size("prop"), lax.axis_size("tx"), lax.axis_size("ty"))
    total_z, total_y, total_x = (planes * n_prop, rows * n_ty, columns * n_tx)
    at_z, at_y, at_x = (lax.axis_index("prop"), lax.axis_index("ty"), lax.axis_index("tx"))
    halo = STEPS
    assert halo <= rows and halo <= columns

    state = jnp.concatenate(
        [
            electric,
            magnetic,
            polarization.reshape((-1,) + electric.shape[1:]),
            current.reshape((-1,) + electric.shape[1:]),
        ],
        axis=0,
    )

    below = -(-STEPS // planes)
    above = -(-(STEPS + STEPS * WSHIFT) // planes)
    whole_column = (below + above + 1) * planes >= total_z
    if whole_column:
        offsets = [k for k in range(-(n_prop - 1), n_prop) if k != 0]
        pieces = from_offsets(state, "prop", offsets)
        pieces[0] = state
        blocks = []
        for j in range(n_prop):
            block = jnp.zeros_like(state)
            for k, piece in pieces.items():
                block = jnp.where(at_z + k == j, piece, block)
            blocks.append(block)
        state = jnp.concatenate(blocks, axis=1)
        base_z = jnp.int32(0)
        own_z = at_z * planes
    else:
        offsets = [k for k in range(-below, above + 1) if k != 0]
        pieces = from_offsets(state, "prop", offsets)
        pieces[0] = state
        state = jnp.concatenate([pieces[k] for k in range(-below, above + 1)], axis=1)
        base_z = (at_z - below) * planes
        own_z = below * planes
    depth = state.shape[1]

    kinds = material.astype(jnp.float32)
    state = jnp.concatenate([state, jnp.broadcast_to(kinds[None, None], (1, depth, rows, columns))], axis=0)
    state = with_halo(state, "tx", 3, halo)
    state = with_halo(state, "ty", 2, halo)
    kinds = state[-1, 0].astype(jnp.int32)
    electric_b, magnetic_b = (state[0:3], state[3:6])
    polarization_b = state[6:12].reshape((2, 3) + state.shape[1:])
    current_b = state[12:18].reshape((2, 3) + state.shape[1:])

    ext_rows, ext_columns = (rows + 2 * halo, columns + 2 * halo)
    keep_mask = (
        inside_range(base_z, depth, total_z, 0, 3)
        & inside_range(at_y * rows - halo, ext_rows, total_y, 1, 3)
        & inside_range(at_x * columns - halo, ext_columns, total_x, 2, 3)
    ).astype(jnp.float32)

    materials_count = permittivity.shape[0]
    selector = kinds[None] == lax.broadcasted_iota(
        jnp.int32, (materials_count, ext_rows, ext_columns), 0
    )
    eps_cell = cell_lookup(selector, permittivity)
    kerr_cell = cell_lookup(selector, nonlinear)
    strength = jnp.stack(
        [cell_lookup(selector, pole_strength[0]), cell_lookup(selector, pole_strength[1])]
    )[:, None, None]
    frequency = jnp.stack(
        [cell_lookup(selector, pole_frequency[0]), cell_lookup(selector, pole_frequency[1])]
    )
    damping = jnp.stack(
        [cell_lookup(selector, pole_damping[0]), cell_lookup(selector, pole_damping[1])]
    )
    half_damp = 0.5 * time_step * damping
    keep_rate = ((1.0 - half_damp) / (1.0 + half_damp))[:, None, None]
    drive_rate = (time_step * frequency * frequency / (1.0 + half_damp))[:, None, None]

    for moment in range(STEPS):
        magnetic_b = (magnetic_b - time_step * curl_forward(electric_b)) * keep_mask[None]
        squared = jnp.sum(electric_b * electric_b, axis=0)
        current_b = keep_rate * current_b + drive_rate * (strength * electric_b[None] - polarization_b)
        polarization_b = polarization_b + time_step * current_b
        electric_b = electric_b + time_step * (
            curl_backward(magnetic_b) - current_b[0] - current_b[1]
        ) / (eps_cell + kerr_cell * squared)
        electric_b = electric_b * keep_mask[None]
        amount = advance[moment]
        electric_b = advance_planes(electric_b, amount, 1)
        magnetic_b = advance_planes(magnetic_b, amount, 1)
        polarization_b = advance_planes(polarization_b, amount, 2)
        current_b = advance_planes(current_b, amount, 2)

    def own(values, dim):
        values = lax.dynamic_slice_in_dim(values, own_z, planes, axis=dim)
        values = lax.slice_in_dim(values, halo, halo + rows, axis=dim + 1)
        return lax.slice_in_dim(values, halo, halo + columns, axis=dim + 2)

    density = eps_cell * jnp.sum(electric_b * electric_b, axis=0) + jnp.sum(
        magnetic_b * magnetic_b, axis=0
    )
    if whole_column:
        column_energy = own(jnp.cumsum(density, axis=0), 0) / jnp.float32(total_z)
    else:
        density = own(density, 0)
        prefix = entering(jnp.sum(density, axis=0), "prop")
        column_energy = (prefix[None] + jnp.cumsum(density, axis=0)) / jnp.float32(total_z)
    return (own(electric_b, 1), own(magnetic_b, 1), own(polarization_b, 2), own(current_b, 2), column_energy)


def solution(mesh):
    return jax.shard_map(
        body,
        mesh=mesh,
        in_specs=(
            P(None, "prop", "ty", "tx"),
            P(None, "prop", "ty", "tx"),
            P(None, None, "prop", "ty", "tx"),
            P(None, None, "prop", "ty", "tx"),
            P("ty", "tx"),
            P(),
            P(),
            P(),
            P(),
            P(),
            P(),
        ),
        out_specs=(
            P(None, "prop", "ty", "tx"),
            P(None, "prop", "ty", "tx"),
            P(None, None, "prop", "ty", "tx"),
            P(None, None, "prop", "ty", "tx"),
            P("prop", "ty", "tx"),
        ),
        check_vma=False,
    )
```

```python
import jax
import jax.numpy as jnp
from jax import lax
from jax.sharding import PartitionSpec as P

STEPS = 4
WSHIFT = 2


time_step = 0.5


def from_offsets(value, axis, offsets):
    count, mine = (lax.axis_size(axis), lax.axis_index(axis))
    got = {}
    for k in offsets:
        if k in got:
            continue
        pairs = [(s, s - k) for s in range(count) if 0 <= s - k < count]
        if not pairs:
            got[k] = jnp.zeros_like(value)
            continue
        if -k in offsets and 2 * abs(k) >= count:
            pairs = pairs + [(s, s + k) for s in range(count) if 0 <= s + k < count]
            received = lax.ppermute(value, axis, pairs)
            for j in (k, -k):
                inside = jnp.logical_and(mine + j >= 0, mine + j < count)
                got[j] = jnp.where(inside, received, jnp.zeros_like(received))
            continue
        got[k] = lax.ppermute(value, axis, pairs)
    return got


def with_halo(cells, axis, dim, width):
    length = cells.shape[dim]
    head = lax.slice_in_dim(cells, 0, width, axis=dim)
    tail = lax.slice_in_dim(cells, length - width, length, axis=dim)
    below = unpacked(from_offsets(packed(tail), axis, (-1,))[-1], tail.shape)
    above = unpacked(from_offsets(packed(head), axis, (1,))[1], head.shape)
    return jnp.concatenate([below, cells, above], axis=dim)


def packed(values):
    lanes = 128
    if values.size % lanes:
        return values.reshape(-1)
    return values.reshape(-1, lanes)


def unpacked(values, shape):
    return values.reshape(shape)


def upper_next(values, dimension):
    zeros_plane = jnp.zeros_like(lax.slice_in_dim(values, 0, 1, axis=dimension))
    rest = lax.slice_in_dim(values, 1, values.shape[dimension], axis=dimension)
    return jnp.concatenate([rest, zeros_plane], axis=dimension)


def lower_next(values, dimension):
    zeros_plane = jnp.zeros_like(lax.slice_in_dim(values, 0, 1, axis=dimension))
    rest = lax.slice_in_dim(values, 0, values.shape[dimension] - 1, axis=dimension)
    return jnp.concatenate([zeros_plane, rest], axis=dimension)


def forward_diff(values, dimension):
    return upper_next(values, dimension) - values


def backward_diff(values, dimension):
    return values - lower_next(values, dimension)


def curl_forward(field):
    field_x, field_y, field_z = field[0], field[1], field[2]
    return jnp.stack([forward_diff(field_z, 1) - forward_diff(field_y, 0),
                      forward_diff(field_x, 0) - forward_diff(field_z, 2),
                      forward_diff(field_y, 2) - forward_diff(field_x, 1)])


def curl_backward(field):
    field_x, field_y, field_z = field[0], field[1], field[2]
    return jnp.stack([backward_diff(field_z, 1) - backward_diff(field_y, 0),
                      backward_diff(field_x, 0) - backward_diff(field_z, 2),
                      backward_diff(field_y, 2) - backward_diff(field_x, 1)])


def advance_planes(values, amount, dimension):
    shape_pad = list(values.shape)
    shape_pad[dimension] = WSHIFT
    joined = jnp.concatenate([values, jnp.zeros(shape_pad, values.dtype)], axis=dimension)
    return lax.dynamic_slice_in_dim(joined, amount, values.shape[dimension], axis=dimension)


def cell_lookup(selector, table):
    return jnp.sum(jnp.where(selector, table[:, None, None], jnp.float32(0.0)), axis=0)


def inside_range(start, length, total, dimension, total_dims):
    shape_one = [1] * total_dims
    shape_one[dimension] = length
    marks = start + lax.broadcasted_iota(jnp.int32, tuple(shape_one), dimension)
    return jnp.logical_and(marks >= 0, marks < total)


def entering(value, axis):
    count, mine = (lax.axis_size(axis), lax.axis_index(axis))
    pieces = lax.all_gather(value, axis)
    running = jnp.zeros_like(value)
    for position in range(count - 1):
        running = jnp.where(position < mine, running + pieces[position], running)
    return running


def body(
    electric,
    magnetic,
    polarization,
    current,
    material,
    advance,
    permittivity,
    nonlinear,
    pole_strength,
    pole_frequency,
    pole_damping,
):
    planes, rows, columns = (electric.shape[1], electric.shape[2], electric.shape[3])
    n_prop, n_tx, n_ty = (lax.axis_size("prop"), lax.axis_size("tx"), lax.axis_size("ty"))
    total_z, total_y, total_x = (planes * n_prop, rows * n_ty, columns * n_tx)
    at_z, at_y, at_x = (lax.axis_index("prop"), lax.axis_index("ty"), lax.axis_index("tx"))
    halo = STEPS
    assert halo <= rows and halo <= columns

    state = jnp.concatenate(
        [
            electric,
            magnetic,
            polarization.reshape((-1,) + electric.shape[1:]),
            current.reshape((-1,) + electric.shape[1:]),
        ],
        axis=0,
    )

    below = -(-STEPS // planes)
    above = -(-(STEPS + STEPS * WSHIFT) // planes)
    whole_column = (below + above + 1) * planes >= total_z
    if whole_column:
        offsets = [k for k in range(-(n_prop - 1), n_prop) if k != 0]
        pieces = from_offsets(state, "prop", offsets)
        pieces[0] = state
        blocks = []
        for j in range(n_prop):
            block = jnp.zeros_like(state)
            for k, piece in pieces.items():
                block = jnp.where(at_z + k == j, piece, block)
            blocks.append(block)
        state = jnp.concatenate(blocks, axis=1)
        base_z = jnp.int32(0)
        own_z = at_z * planes
    else:
        offsets = [k for k in range(-below, above + 1) if k != 0]
        pieces = from_offsets(state, "prop", offsets)
        pieces[0] = state
        state = jnp.concatenate([pieces[k] for k in range(-below, above + 1)], axis=1)
        base_z = (at_z - below) * planes
        own_z = below * planes
    depth = state.shape[1]

    kinds = material.astype(jnp.float32)
    state = jnp.concatenate([state, jnp.broadcast_to(kinds[None, None], (1, depth, rows, columns))], axis=0)
    state = with_halo(state, "tx", 3, halo)
    state = with_halo(state, "ty", 2, halo)
    kinds = state[-1, 0].astype(jnp.int32)
    electric_b, magnetic_b = (state[0:3], state[3:6])
    polarization_b = state[6:12].reshape((2, 3) + state.shape[1:])
    current_b = state[12:18].reshape((2, 3) + state.shape[1:])

    ext_rows, ext_columns = (rows + 2 * halo, columns + 2 * halo)
    keep_mask = (
        inside_range(base_z, depth, total_z, 0, 3)
        & inside_range(at_y * rows - halo, ext_rows, total_y, 1, 3)
        & inside_range(at_x * columns - halo, ext_columns, total_x, 2, 3)
    ).astype(jnp.float32)

    materials_count = permittivity.shape[0]
    selector = kinds[None] == lax.broadcasted_iota(
        jnp.int32, (materials_count, ext_rows, ext_columns), 0
    )
    eps_cell = cell_lookup(selector, permittivity)
    kerr_cell = cell_lookup(selector, nonlinear)
    strength = jnp.stack(
        [cell_lookup(selector, pole_strength[0]), cell_lookup(selector, pole_strength[1])]
    )[:, None, None]
    frequency = jnp.stack(
        [cell_lookup(selector, pole_frequency[0]), cell_lookup(selector, pole_frequency[1])]
    )
    damping = jnp.stack(
        [cell_lookup(selector, pole_damping[0]), cell_lookup(selector, pole_damping[1])]
    )
    half_damp = 0.5 * time_step * damping
    keep_rate = ((1.0 - half_damp) / (1.0 + half_damp))[:, None, None]
    drive_rate = (time_step * frequency * frequency / (1.0 + half_damp))[:, None, None]

    for moment in range(STEPS):
        magnetic_b = (magnetic_b - time_step * curl_forward(electric_b)) * keep_mask[None]
        squared = jnp.sum(electric_b * electric_b, axis=0)
        current_b = keep_rate * current_b + drive_rate * (strength * electric_b[None] - polarization_b)
        polarization_b = polarization_b + time_step * current_b
        electric_b = electric_b + time_step * (
            curl_backward(magnetic_b) - current_b[0] - current_b[1]
        ) / (eps_cell + kerr_cell * squared)
        electric_b = electric_b * keep_mask[None]
        amount = advance[moment]
        electric_b = advance_planes(electric_b, amount, 1)
        magnetic_b = advance_planes(magnetic_b, amount, 1)
        polarization_b = advance_planes(polarization_b, amount, 2)
        current_b = advance_planes(current_b, amount, 2)

    def own(values, dim):
        values = lax.dynamic_slice_in_dim(values, own_z, planes, axis=dim)
        values = lax.slice_in_dim(values, halo, halo + rows, axis=dim + 1)
        return lax.slice_in_dim(values, halo, halo + columns, axis=dim + 2)

    density = eps_cell * jnp.sum(electric_b * electric_b, axis=0) + jnp.sum(
        magnetic_b * magnetic_b, axis=0
    )
    if whole_column:
        column_energy = own(jnp.cumsum(density, axis=0), 0) / jnp.float32(total_z)
    else:
        density = own(density, 0)
        prefix = entering(jnp.sum(density, axis=0), "prop")
        column_energy = (prefix[None] + jnp.cumsum(density, axis=0)) / jnp.float32(total_z)
    return (own(electric_b, 1), own(magnetic_b, 1), own(polarization_b, 2), own(current_b, 2), column_energy)


def solution(mesh):
    return jax.shard_map(
        body,
        mesh=mesh,
        in_specs=(
            P(None, "prop", "ty", "tx"),
            P(None, "prop", "ty", "tx"),
            P(None, None, "prop", "ty", "tx"),
            P(None, None, "prop", "ty", "tx"),
            P("ty", "tx"),
            P(),
            P(),
            P(),
            P(),
            P(),
            P(),
        ),
        out_specs=(
            P(None, "prop", "ty", "tx"),
            P(None, "prop", "ty", "tx"),
            P(None, None, "prop", "ty", "tx"),
            P(None, None, "prop", "ty", "tx"),
            P("prop", "ty", "tx"),
        ),
        check_vma=False,
    )
```

```python
import jax
import jax.numpy as jnp
from jax import lax
from jax.sharding import PartitionSpec as P

STEPS = 4
WSHIFT = 2


time_step = 0.5


def from_offsets(value, axis, offsets):
    count, mine = (lax.axis_size(axis), lax.axis_index(axis))
    got = {}
    for k in offsets:
        if k in got:
            continue
        pairs = [(s, s - k) for s in range(count) if 0 <= s - k < count]
        if not pairs:
            got[k] = jnp.zeros_like(value)
            continue
        if -k in offsets and 2 * abs(k) >= count:
            pairs = pairs + [(s, s + k) for s in range(count) if 0 <= s + k < count]
            received = lax.ppermute(value, axis, pairs)
            for j in (k, -k):
                inside = jnp.logical_and(mine + j >= 0, mine + j < count)
                got[j] = jnp.where(inside, received, jnp.zeros_like(received))
            continue
        got[k] = lax.ppermute(value, axis, pairs)
    return got


def from_neighbours(value_for, axes, offsets):
    counts = [lax.axis_size(a) for a in axes]
    mine = [lax.axis_index(a) for a in axes]
    coords = [()]
    for n in counts:
        coords = [c + (i,) for c in coords for i in range(n)]

    def linear(c):
        index = 0
        for i, n in zip(c, counts):
            index = index * n + i
        return index

    def pairs_of(k):
        out = []
        for c in coords:
            t = tuple(ci - ki for ci, ki in zip(c, k))
            if all(0 <= ti < n for ti, n in zip(t, counts)):
                out.append((linear(c), linear(t)))
        return out

    def exists(k):
        ok = jnp.bool_(True)
        for m, ki, n in zip(mine, k, counts):
            ok = ok & (m + ki >= 0) & (m + ki < n)
        return ok

    got = {}
    for k in offsets:
        if k in got:
            continue
        back = tuple(-ki for ki in k)
        pairs = pairs_of(k)
        if not pairs:
            got[k] = jnp.zeros_like(value_for(back))
            continue
        if back in offsets and back not in got:
            both = pairs + pairs_of(back)
            if len({a for a, _ in both}) == len(both) and len({b for _, b in both}) == len(both):
                toward_back, toward_k = (value_for(back), value_for(k))
                payload = toward_k
                if toward_back is not toward_k:
                    payload = jnp.where(exists(back), toward_back, toward_k)
                received = lax.ppermute(payload, axes, both)
                for j in (k, back):
                    got[j] = jnp.where(exists(j), received, jnp.zeros_like(received))
                continue
        got[k] = lax.ppermute(value_for(back), axes, pairs)
    return got


def with_halo(cells, axis, dim, width):
    length = cells.shape[dim]
    head = lax.slice_in_dim(cells, 0, width, axis=dim)
    tail = lax.slice_in_dim(cells, length - width, length, axis=dim)
    below = unpacked(from_offsets(packed(tail), axis, (-1,))[-1], tail.shape)
    above = unpacked(from_offsets(packed(head), axis, (1,))[1], head.shape)
    return jnp.concatenate([below, cells, above], axis=dim)


def packed(values):
    lanes = 128
    if values.size % lanes:
        return values.reshape(-1)
    return values.reshape(-1, lanes)


def unpacked(values, shape):
    return values.reshape(shape)


def upper_next(values, dimension):
    zeros_plane = jnp.zeros_like(lax.slice_in_dim(values, 0, 1, axis=dimension))
    rest = lax.slice_in_dim(values, 1, values.shape[dimension], axis=dimension)
    return jnp.concatenate([rest, zeros_plane], axis=dimension)


def lower_next(values, dimension):
    zeros_plane = jnp.zeros_like(lax.slice_in_dim(values, 0, 1, axis=dimension))
    rest = lax.slice_in_dim(values, 0, values.shape[dimension] - 1, axis=dimension)
    return jnp.concatenate([zeros_plane, rest], axis=dimension)


def forward_diff(values, dimension):
    return upper_next(values, dimension) - values


def backward_diff(values, dimension):
    return values - lower_next(values, dimension)


def curl_forward(field):
    field_x, field_y, field_z = field[0], field[1], field[2]
    return jnp.stack([forward_diff(field_z, 1) - forward_diff(field_y, 0),
                      forward_diff(field_x, 0) - forward_diff(field_z, 2),
                      forward_diff(field_y, 2) - forward_diff(field_x, 1)])


def curl_backward(field):
    field_x, field_y, field_z = field[0], field[1], field[2]
    return jnp.stack([backward_diff(field_z, 1) - backward_diff(field_y, 0),
                      backward_diff(field_x, 0) - backward_diff(field_z, 2),
                      backward_diff(field_y, 2) - backward_diff(field_x, 1)])


def advance_planes(values, amount, dimension):
    shape_pad = list(values.shape)
    shape_pad[dimension] = WSHIFT
    joined = jnp.concatenate([values, jnp.zeros(shape_pad, values.dtype)], axis=dimension)
    return lax.dynamic_slice_in_dim(joined, amount, values.shape[dimension], axis=dimension)


def cell_lookup(selector, table):
    return jnp.sum(jnp.where(selector, table[:, None, None], jnp.float32(0.0)), axis=0)


def inside_range(start, length, total, dimension, total_dims):
    shape_one = [1] * total_dims
    shape_one[dimension] = length
    marks = start + lax.broadcasted_iota(jnp.int32, tuple(shape_one), dimension)
    return jnp.logical_and(marks >= 0, marks < total)


def entering(value, axis):
    count, mine = (lax.axis_size(axis), lax.axis_index(axis))
    pieces = lax.all_gather(value, axis)
    running = jnp.zeros_like(value)
    for position in range(count - 1):
        running = jnp.where(position < mine, running + pieces[position], running)
    return running


def body(
    electric,
    magnetic,
    polarization,
    current,
    material,
    advance,
    permittivity,
    nonlinear,
    pole_strength,
    pole_frequency,
    pole_damping,
):
    planes, rows, columns = (electric.shape[1], electric.shape[2], electric.shape[3])
    n_prop, n_tx, n_ty = (lax.axis_size("prop"), lax.axis_size("tx"), lax.axis_size("ty"))
    total_z, total_y, total_x = (planes * n_prop, rows * n_ty, columns * n_tx)
    at_z, at_y, at_x = (lax.axis_index("prop"), lax.axis_index("ty"), lax.axis_index("tx"))
    halo = STEPS
    assert halo <= rows and halo <= columns

    state = jnp.concatenate(
        [
            electric,
            magnetic,
            polarization.reshape((-1,) + electric.shape[1:]),
            current.reshape((-1,) + electric.shape[1:]),
        ],
        axis=0,
    )

    below = -(-STEPS // planes)
    above = -(-(STEPS + STEPS * WSHIFT) // planes)
    whole_column = (below + above + 1) * planes >= total_z
    kinds = material.astype(jnp.float32)
    with_kinds = jnp.concatenate([state, jnp.broadcast_to(kinds[None, None], (1,) + state.shape[1:])], axis=0)
    if whole_column:
        head = lax.slice_in_dim(with_kinds, 0, halo, axis=3)
        tail = lax.slice_in_dim(with_kinds, columns - halo, columns, axis=3)

        def value_for(d):
            if d[1] == 0:
                return state
            return packed(tail if d[1] > 0 else head)

        offsets = [
            (kz, kx) for kz in range(-(n_prop - 1), n_prop) for kx in (-1, 0, 1) if (kz, kx) != (0, 0)
        ]
        pieces = from_neighbours(value_for, ("prop", "tx"), offsets)
        pieces[(0, 0)] = state
        blocks = []
        for j in range(n_prop):
            parts = []
            for kx in (-1, 0, 1):
                part = None
                for kz in range(-(n_prop - 1), n_prop):
                    piece = pieces[(kz, kx)]
                    part = piece if part is None else jnp.where(at_z + kz == j, piece, part)
                if kx == 0:
                    part = jnp.concatenate([part, with_kinds[-1:]], axis=0)
                else:
                    part = unpacked(part, head.shape)
                parts.append(part)
            blocks.append(jnp.concatenate(parts, axis=3))
        state = jnp.concatenate(blocks, axis=1)
        base_z = jnp.int32(0)
        own_z = at_z * planes
    else:
        offsets = [k for k in range(-below, above + 1) if k != 0]
        pieces = from_offsets(with_kinds, "prop", offsets)
        pieces[0] = with_kinds
        state = jnp.concatenate([pieces[k] for k in range(-below, above + 1)], axis=1)
        base_z = (at_z - below) * planes
        own_z = below * planes
        state = with_halo(state, "tx", 3, halo)
    depth = state.shape[1]
    state = with_halo(state, "ty", 2, halo)
    kinds = state[-1, 0].astype(jnp.int32)
    electric_b, magnetic_b = (state[0:3], state[3:6])
    polarization_b = state[6:12].reshape((2, 3) + state.shape[1:])
    current_b = state[12:18].reshape((2, 3) + state.shape[1:])

    ext_rows, ext_columns = (rows + 2 * halo, columns + 2 * halo)
    keep_mask = (
        inside_range(base_z, depth, total_z, 0, 3)
        & inside_range(at_y * rows - halo, ext_rows, total_y, 1, 3)
        & inside_range(at_x * columns - halo, ext_columns, total_x, 2, 3)
    ).astype(jnp.float32)

    materials_count = permittivity.shape[0]
    selector = kinds[None] == lax.broadcasted_iota(
        jnp.int32, (materials_count, ext_rows, ext_columns), 0
    )
    eps_cell = cell_lookup(selector, permittivity)
    kerr_cell = cell_lookup(selector, nonlinear)
    strength = jnp.stack(
        [cell_lookup(selector, pole_strength[0]), cell_lookup(selector, pole_strength[1])]
    )[:, None, None]
    frequency = jnp.stack(
        [cell_lookup(selector, pole_frequency[0]), cell_lookup(selector, pole_frequency[1])]
    )
    damping = jnp.stack(
        [cell_lookup(selector, pole_damping[0]), cell_lookup(selector, pole_damping[1])]
    )
    half_damp = 0.5 * time_step * damping
    keep_rate = ((1.0 - half_damp) / (1.0 + half_damp))[:, None, None]
    drive_rate = (time_step * frequency * frequency / (1.0 + half_damp))[:, None, None]

    for moment in range(STEPS):
        magnetic_b = (magnetic_b - time_step * curl_forward(electric_b)) * keep_mask[None]
        squared = jnp.sum(electric_b * electric_b, axis=0)
        current_b = keep_rate * current_b + drive_rate * (strength * electric_b[None] - polarization_b)
        polarization_b = polarization_b + time_step * current_b
        electric_b = electric_b + time_step * (
            curl_backward(magnetic_b) - current_b[0] - current_b[1]
        ) / (eps_cell + kerr_cell * squared)
        electric_b = electric_b * keep_mask[None]
        amount = advance[moment]
        electric_b = advance_planes(electric_b, amount, 1)
        magnetic_b = advance_planes(magnetic_b, amount, 1)
        polarization_b = advance_planes(polarization_b, amount, 2)
        current_b = advance_planes(current_b, amount, 2)

    def own(values, dim):
        values = lax.dynamic_slice_in_dim(values, own_z, planes, axis=dim)
        values = lax.slice_in_dim(values, halo, halo + rows, axis=dim + 1)
        return lax.slice_in_dim(values, halo, halo + columns, axis=dim + 2)

    density = eps_cell * jnp.sum(electric_b * electric_b, axis=0) + jnp.sum(
        magnetic_b * magnetic_b, axis=0
    )
    if whole_column:
        column_energy = own(jnp.cumsum(density, axis=0), 0) / jnp.float32(total_z)
    else:
        density = own(density, 0)
        prefix = entering(jnp.sum(density, axis=0), "prop")
        column_energy = (prefix[None] + jnp.cumsum(density, axis=0)) / jnp.float32(total_z)
    return (own(electric_b, 1), own(magnetic_b, 1), own(polarization_b, 2), own(current_b, 2), column_energy)


def solution(mesh):
    return jax.shard_map(
        body,
        mesh=mesh,
        in_specs=(
            P(None, "prop", "ty", "tx"),
            P(None, "prop", "ty", "tx"),
            P(None, None, "prop", "ty", "tx"),
            P(None, None, "prop", "ty", "tx"),
            P("ty", "tx"),
            P(),
            P(),
            P(),
            P(),
            P(),
            P(),
        ),
        out_specs=(
            P(None, "prop", "ty", "tx"),
            P(None, "prop", "ty", "tx"),
            P(None, None, "prop", "ty", "tx"),
            P(None, None, "prop", "ty", "tx"),
            P("prop", "ty", "tx"),
        ),
        check_vma=False,
    )
```

```python
import jax
import jax.numpy as jnp
from jax import lax
from jax.sharding import PartitionSpec as P

STEPS = 4
WSHIFT = 2


time_step = 0.5


def from_offsets(value, axis, offsets):
    count, mine = (lax.axis_size(axis), lax.axis_index(axis))
    got = {}
    for k in offsets:
        if k in got:
            continue
        pairs = [(s, s - k) for s in range(count) if 0 <= s - k < count]
        if not pairs:
            got[k] = jnp.zeros_like(value)
            continue
        if -k in offsets and 2 * abs(k) >= count:
            pairs = pairs + [(s, s + k) for s in range(count) if 0 <= s + k < count]
            received = lax.ppermute(value, axis, pairs)
            for j in (k, -k):
                inside = jnp.logical_and(mine + j >= 0, mine + j < count)
                got[j] = jnp.where(inside, received, jnp.zeros_like(received))
            continue
        got[k] = lax.ppermute(value, axis, pairs)
    return got


def with_halo(cells, axis, dim, width):
    length = cells.shape[dim]
    head = lax.slice_in_dim(cells, 0, width, axis=dim)
    tail = lax.slice_in_dim(cells, length - width, length, axis=dim)
    below = unpacked(from_offsets(packed(tail), axis, (-1,))[-1], tail.shape)
    above = unpacked(from_offsets(packed(head), axis, (1,))[1], head.shape)
    return jnp.concatenate([below, cells, above], axis=dim)


def packed(values):
    lanes = 128
    if values.size % lanes:
        return values.reshape(-1)
    return values.reshape(-1, lanes)


def unpacked(values, shape):
    return values.reshape(shape)


def upper_next(values, dimension):
    zeros_plane = jnp.zeros_like(lax.slice_in_dim(values, 0, 1, axis=dimension))
    rest = lax.slice_in_dim(values, 1, values.shape[dimension], axis=dimension)
    return jnp.concatenate([rest, zeros_plane], axis=dimension)


def lower_next(values, dimension):
    zeros_plane = jnp.zeros_like(lax.slice_in_dim(values, 0, 1, axis=dimension))
    rest = lax.slice_in_dim(values, 0, values.shape[dimension] - 1, axis=dimension)
    return jnp.concatenate([zeros_plane, rest], axis=dimension)


def forward_diff(values, dimension):
    return upper_next(values, dimension) - values


def backward_diff(values, dimension):
    return values - lower_next(values, dimension)


def curl_forward(field):
    field_x, field_y, field_z = field[0], field[1], field[2]
    return jnp.stack([forward_diff(field_z, 1) - forward_diff(field_y, 0),
                      forward_diff(field_x, 0) - forward_diff(field_z, 2),
                      forward_diff(field_y, 2) - forward_diff(field_x, 1)])


def curl_backward(field):
    field_x, field_y, field_z = field[0], field[1], field[2]
    return jnp.stack([backward_diff(field_z, 1) - backward_diff(field_y, 0),
                      backward_diff(field_x, 0) - backward_diff(field_z, 2),
                      backward_diff(field_y, 2) - backward_diff(field_x, 1)])


def advance_planes(values, amount, dimension):
    shape_pad = list(values.shape)
    shape_pad[dimension] = WSHIFT
    joined = jnp.concatenate([values, jnp.zeros(shape_pad, values.dtype)], axis=dimension)
    return lax.dynamic_slice_in_dim(joined, amount, values.shape[dimension], axis=dimension)


def cell_lookup(selector, table):
    return jnp.sum(jnp.where(selector, table[:, None, None], jnp.float32(0.0)), axis=0)


def inside_range(start, length, total, dimension, total_dims):
    shape_one = [1] * total_dims
    shape_one[dimension] = length
    marks = start + lax.broadcasted_iota(jnp.int32, tuple(shape_one), dimension)
    return jnp.logical_and(marks >= 0, marks < total)


def entering(value, axis):
    count, mine = (lax.axis_size(axis), lax.axis_index(axis))
    pieces = lax.all_gather(value, axis)
    running = jnp.zeros_like(value)
    for position in range(count - 1):
        running = jnp.where(position < mine, running + pieces[position], running)
    return running


def body(
    electric,
    magnetic,
    polarization,
    current,
    material,
    advance,
    permittivity,
    nonlinear,
    pole_strength,
    pole_frequency,
    pole_damping,
):
    planes, rows, columns = (electric.shape[1], electric.shape[2], electric.shape[3])
    n_prop, n_tx, n_ty = (lax.axis_size("prop"), lax.axis_size("tx"), lax.axis_size("ty"))
    total_z, total_y, total_x = (planes * n_prop, rows * n_ty, columns * n_tx)
    at_z, at_y, at_x = (lax.axis_index("prop"), lax.axis_index("ty"), lax.axis_index("tx"))
    halo = STEPS
    assert halo <= rows and halo <= columns

    state = jnp.concatenate(
        [
            electric,
            magnetic,
            polarization.reshape((-1,) + electric.shape[1:]),
            current.reshape((-1,) + electric.shape[1:]),
        ],
        axis=0,
    )

    below = -(-STEPS // planes)
    above = -(-(STEPS + STEPS * WSHIFT) // planes)
    whole_column = (below + above + 1) * planes >= total_z
    if whole_column:
        offsets = [k for k in range(-(n_prop - 1), n_prop) if k != 0]
        pieces = from_offsets(state, "prop", offsets)
        pieces[0] = state
        blocks = []
        for j in range(n_prop):
            block = jnp.zeros_like(state)
            for k, piece in pieces.items():
                block = jnp.where(at_z + k == j, piece, block)
            blocks.append(block)
        state = jnp.concatenate(blocks, axis=1)
        base_z = jnp.int32(0)
        own_z = at_z * planes
    else:
        offsets = [k for k in range(-below, above + 1) if k != 0]
        pieces = from_offsets(state, "prop", offsets)
        pieces[0] = state
        state = jnp.concatenate([pieces[k] for k in range(-below, above + 1)], axis=1)
        base_z = (at_z - below) * planes
        own_z = below * planes
    depth = state.shape[1]

    kinds = material.astype(jnp.float32)
    state = jnp.concatenate([state, jnp.broadcast_to(kinds[None, None], (1, depth, rows, columns))], axis=0)
    state = with_halo(state, "ty", 2, halo)
    state = with_halo(state, "tx", 3, halo)
    kinds = state[-1, 0].astype(jnp.int32)
    electric_b, magnetic_b = (state[0:3], state[3:6])
    polarization_b = state[6:12].reshape((2, 3) + state.shape[1:])
    current_b = state[12:18].reshape((2, 3) + state.shape[1:])

    ext_rows, ext_columns = (rows + 2 * halo, columns + 2 * halo)
    keep_mask = (
        inside_range(base_z, depth, total_z, 0, 3)
        & inside_range(at_y * rows - halo, ext_rows, total_y, 1, 3)
        & inside_range(at_x * columns - halo, ext_columns, total_x, 2, 3)
    ).astype(jnp.float32)

    materials_count = permittivity.shape[0]
    selector = kinds[None] == lax.broadcasted_iota(
        jnp.int32, (materials_count, ext_rows, ext_columns), 0
    )
    eps_cell = cell_lookup(selector, permittivity)
    kerr_cell = cell_lookup(selector, nonlinear)
    strength = jnp.stack(
        [cell_lookup(selector, pole_strength[0]), cell_lookup(selector, pole_strength[1])]
    )[:, None, None]
    frequency = jnp.stack(
        [cell_lookup(selector, pole_frequency[0]), cell_lookup(selector, pole_frequency[1])]
    )
    damping = jnp.stack(
        [cell_lookup(selector, pole_damping[0]), cell_lookup(selector, pole_damping[1])]
    )
    half_damp = 0.5 * time_step * damping
    keep_rate = ((1.0 - half_damp) / (1.0 + half_damp))[:, None, None]
    drive_rate = (time_step * frequency * frequency / (1.0 + half_damp))[:, None, None]

    for moment in range(STEPS):
        magnetic_b = (magnetic_b - time_step * curl_forward(electric_b)) * keep_mask[None]
        squared = jnp.sum(electric_b * electric_b, axis=0)
        current_b = keep_rate * current_b + drive_rate * (strength * electric_b[None] - polarization_b)
        polarization_b = polarization_b + time_step * current_b
        electric_b = electric_b + time_step * (
            curl_backward(magnetic_b) - current_b[0] - current_b[1]
        ) / (eps_cell + kerr_cell * squared)
        electric_b = electric_b * keep_mask[None]
        amount = advance[moment]
        electric_b = advance_planes(electric_b, amount, 1)
        magnetic_b = advance_planes(magnetic_b, amount, 1)
        polarization_b = advance_planes(polarization_b, amount, 2)
        current_b = advance_planes(current_b, amount, 2)

    def own(values, dim):
        values = lax.dynamic_slice_in_dim(values, own_z, planes, axis=dim)
        values = lax.slice_in_dim(values, halo, halo + rows, axis=dim + 1)
        return lax.slice_in_dim(values, halo, halo + columns, axis=dim + 2)

    density = eps_cell * jnp.sum(electric_b * electric_b, axis=0) + jnp.sum(
        magnetic_b * magnetic_b, axis=0
    )
    if whole_column:
        column_energy = own(jnp.cumsum(density, axis=0), 0) / jnp.float32(total_z)
    else:
        density = own(density, 0)
        prefix = entering(jnp.sum(density, axis=0), "prop")
        column_energy = (prefix[None] + jnp.cumsum(density, axis=0)) / jnp.float32(total_z)
    return (own(electric_b, 1), own(magnetic_b, 1), own(polarization_b, 2), own(current_b, 2), column_energy)


def solution(mesh):
    return jax.shard_map(
        body,
        mesh=mesh,
        in_specs=(
            P(None, "prop", "ty", "tx"),
            P(None, "prop", "ty", "tx"),
            P(None, None, "prop", "ty", "tx"),
            P(None, None, "prop", "ty", "tx"),
            P("ty", "tx"),
            P(),
            P(),
            P(),
            P(),
            P(),
            P(),
        ),
        out_specs=(
            P(None, "prop", "ty", "tx"),
            P(None, "prop", "ty", "tx"),
            P(None, None, "prop", "ty", "tx"),
            P(None, None, "prop", "ty", "tx"),
            P("prop", "ty", "tx"),
        ),
        check_vma=False,
    )
```

```python
import jax
import jax.numpy as jnp
from jax import lax
from jax.sharding import PartitionSpec as P

STEPS = 4
WSHIFT = 2


time_step = 0.5


def from_offsets(value, axis, offsets):
    count, mine = (lax.axis_size(axis), lax.axis_index(axis))
    got = {}
    for k in offsets:
        if k in got:
            continue
        pairs = [(s, s - k) for s in range(count) if 0 <= s - k < count]
        if not pairs:
            got[k] = jnp.zeros_like(value)
            continue
        if -k in offsets and 2 * abs(k) >= count:
            pairs = pairs + [(s, s + k) for s in range(count) if 0 <= s + k < count]
            received = lax.ppermute(value, axis, pairs)
            for j in (k, -k):
                inside = jnp.logical_and(mine + j >= 0, mine + j < count)
                got[j] = jnp.where(inside, received, jnp.zeros_like(received))
            continue
        got[k] = lax.ppermute(value, axis, pairs)
    return got


def with_halo(cells, axis, dim, width):
    length = cells.shape[dim]
    head = lax.slice_in_dim(cells, 0, width, axis=dim)
    tail = lax.slice_in_dim(cells, length - width, length, axis=dim)
    if dim == cells.ndim - 1:
        def pack(values):
            return values.reshape(-1, width).T

        def unpack(values, shape):
            return values.T.reshape(shape)
    else:
        pack, unpack = (packed, unpacked)
    below = unpack(from_offsets(pack(tail), axis, (-1,))[-1], tail.shape)
    above = unpack(from_offsets(pack(head), axis, (1,))[1], head.shape)
    return jnp.concatenate([below, cells, above], axis=dim)


def packed(values):
    lanes = 128
    if values.size % lanes:
        return values.reshape(-1)
    return values.reshape(-1, lanes)


def unpacked(values, shape):
    return values.reshape(shape)


def upper_next(values, dimension):
    zeros_plane = jnp.zeros_like(lax.slice_in_dim(values, 0, 1, axis=dimension))
    rest = lax.slice_in_dim(values, 1, values.shape[dimension], axis=dimension)
    return jnp.concatenate([rest, zeros_plane], axis=dimension)


def lower_next(values, dimension):
    zeros_plane = jnp.zeros_like(lax.slice_in_dim(values, 0, 1, axis=dimension))
    rest = lax.slice_in_dim(values, 0, values.shape[dimension] - 1, axis=dimension)
    return jnp.concatenate([zeros_plane, rest], axis=dimension)


def forward_diff(values, dimension):
    return upper_next(values, dimension) - values


def backward_diff(values, dimension):
    return values - lower_next(values, dimension)


def curl_forward(field):
    field_x, field_y, field_z = field[0], field[1], field[2]
    return jnp.stack([forward_diff(field_z, 1) - forward_diff(field_y, 0),
                      forward_diff(field_x, 0) - forward_diff(field_z, 2),
                      forward_diff(field_y, 2) - forward_diff(field_x, 1)])


def curl_backward(field):
    field_x, field_y, field_z = field[0], field[1], field[2]
    return jnp.stack([backward_diff(field_z, 1) - backward_diff(field_y, 0),
                      backward_diff(field_x, 0) - backward_diff(field_z, 2),
                      backward_diff(field_y, 2) - backward_diff(field_x, 1)])


def advance_planes(values, amount, dimension):
    shape_pad = list(values.shape)
    shape_pad[dimension] = WSHIFT
    joined = jnp.concatenate([values, jnp.zeros(shape_pad, values.dtype)], axis=dimension)
    return lax.dynamic_slice_in_dim(joined, amount, values.shape[dimension], axis=dimension)


def cell_lookup(selector, table):
    return jnp.sum(jnp.where(selector, table[:, None, None], jnp.float32(0.0)), axis=0)


def inside_range(start, length, total, dimension, total_dims):
    shape_one = [1] * total_dims
    shape_one[dimension] = length
    marks = start + lax.broadcasted_iota(jnp.int32, tuple(shape_one), dimension)
    return jnp.logical_and(marks >= 0, marks < total)


def entering(value, axis):
    count, mine = (lax.axis_size(axis), lax.axis_index(axis))
    pieces = lax.all_gather(value, axis)
    running = jnp.zeros_like(value)
    for position in range(count - 1):
        running = jnp.where(position < mine, running + pieces[position], running)
    return running


def body(
    electric,
    magnetic,
    polarization,
    current,
    material,
    advance,
    permittivity,
    nonlinear,
    pole_strength,
    pole_frequency,
    pole_damping,
):
    planes, rows, columns = (electric.shape[1], electric.shape[2], electric.shape[3])
    n_prop, n_tx, n_ty = (lax.axis_size("prop"), lax.axis_size("tx"), lax.axis_size("ty"))
    total_z, total_y, total_x = (planes * n_prop, rows * n_ty, columns * n_tx)
    at_z, at_y, at_x = (lax.axis_index("prop"), lax.axis_index("ty"), lax.axis_index("tx"))
    halo = STEPS
    assert halo <= rows and halo <= columns

    state = jnp.concatenate(
        [
            electric,
            magnetic,
            polarization.reshape((-1,) + electric.shape[1:]),
            current.reshape((-1,) + electric.shape[1:]),
        ],
        axis=0,
    )

    below = -(-STEPS // planes)
    above = -(-(STEPS + STEPS * WSHIFT) // planes)
    whole_column = (below + above + 1) * planes >= total_z
    if whole_column:
        offsets = [k for k in range(-(n_prop - 1), n_prop) if k != 0]
        pieces = from_offsets(state, "prop", offsets)
        pieces[0] = state
        blocks = []
        for j in range(n_prop):
            block = jnp.zeros_like(state)
            for k, piece in pieces.items():
                block = jnp.where(at_z + k == j, piece, block)
            blocks.append(block)
        state = jnp.concatenate(blocks, axis=1)
        base_z = jnp.int32(0)
        own_z = at_z * planes
    else:
        offsets = [k for k in range(-below, above + 1) if k != 0]
        pieces = from_offsets(state, "prop", offsets)
        pieces[0] = state
        state = jnp.concatenate([pieces[k] for k in range(-below, above + 1)], axis=1)
        base_z = (at_z - below) * planes
        own_z = below * planes
    depth = state.shape[1]

    kinds = material.astype(jnp.float32)
    state = jnp.concatenate([state, jnp.broadcast_to(kinds[None, None], (1, depth, rows, columns))], axis=0)
    state = with_halo(state, "ty", 2, halo)
    state = with_halo(state, "tx", 3, halo)
    kinds = state[-1, 0].astype(jnp.int32)
    electric_b, magnetic_b = (state[0:3], state[3:6])
    polarization_b = state[6:12].reshape((2, 3) + state.shape[1:])
    current_b = state[12:18].reshape((2, 3) + state.shape[1:])

    ext_rows, ext_columns = (rows + 2 * halo, columns + 2 * halo)
    keep_mask = (
        inside_range(base_z, depth, total_z, 0, 3)
        & inside_range(at_y * rows - halo, ext_rows, total_y, 1, 3)
        & inside_range(at_x * columns - halo, ext_columns, total_x, 2, 3)
    ).astype(jnp.float32)

    materials_count = permittivity.shape[0]
    selector = kinds[None] == lax.broadcasted_iota(
        jnp.int32, (materials_count, ext_rows, ext_columns), 0
    )
    eps_cell = cell_lookup(selector, permittivity)
    kerr_cell = cell_lookup(selector, nonlinear)
    strength = jnp.stack(
        [cell_lookup(selector, pole_strength[0]), cell_lookup(selector, pole_strength[1])]
    )[:, None, None]
    frequency = jnp.stack(
        [cell_lookup(selector, pole_frequency[0]), cell_lookup(selector, pole_frequency[1])]
    )
    damping = jnp.stack(
        [cell_lookup(selector, pole_damping[0]), cell_lookup(selector, pole_damping[1])]
    )
    half_damp = 0.5 * time_step * damping
    keep_rate = ((1.0 - half_damp) / (1.0 + half_damp))[:, None, None]
    drive_rate = (time_step * frequency * frequency / (1.0 + half_damp))[:, None, None]

    for moment in range(STEPS):
        magnetic_b = (magnetic_b - time_step * curl_forward(electric_b)) * keep_mask[None]
        squared = jnp.sum(electric_b * electric_b, axis=0)
        current_b = keep_rate * current_b + drive_rate * (strength * electric_b[None] - polarization_b)
        polarization_b = polarization_b + time_step * current_b
        electric_b = electric_b + time_step * (
            curl_backward(magnetic_b) - current_b[0] - current_b[1]
        ) / (eps_cell + kerr_cell * squared)
        electric_b = electric_b * keep_mask[None]
        amount = advance[moment]
        electric_b = advance_planes(electric_b, amount, 1)
        magnetic_b = advance_planes(magnetic_b, amount, 1)
        polarization_b = advance_planes(polarization_b, amount, 2)
        current_b = advance_planes(current_b, amount, 2)

    def own(values, dim):
        values = lax.dynamic_slice_in_dim(values, own_z, planes, axis=dim)
        values = lax.slice_in_dim(values, halo, halo + rows, axis=dim + 1)
        return lax.slice_in_dim(values, halo, halo + columns, axis=dim + 2)

    density = eps_cell * jnp.sum(electric_b * electric_b, axis=0) + jnp.sum(
        magnetic_b * magnetic_b, axis=0
    )
    if whole_column:
        column_energy = own(jnp.cumsum(density, axis=0), 0) / jnp.float32(total_z)
    else:
        density = own(density, 0)
        prefix = entering(jnp.sum(density, axis=0), "prop")
        column_energy = (prefix[None] + jnp.cumsum(density, axis=0)) / jnp.float32(total_z)
    return (own(electric_b, 1), own(magnetic_b, 1), own(polarization_b, 2), own(current_b, 2), column_energy)


def solution(mesh):
    return jax.shard_map(
        body,
        mesh=mesh,
        in_specs=(
            P(None, "prop", "ty", "tx"),
            P(None, "prop", "ty", "tx"),
            P(None, None, "prop", "ty", "tx"),
            P(None, None, "prop", "ty", "tx"),
            P("ty", "tx"),
            P(),
            P(),
            P(),
            P(),
            P(),
            P(),
        ),
        out_specs=(
            P(None, "prop", "ty", "tx"),
            P(None, "prop", "ty", "tx"),
            P(None, None, "prop", "ty", "tx"),
            P(None, None, "prop", "ty", "tx"),
            P("prop", "ty", "tx"),
        ),
        check_vma=False,
    )
```

```python
import functools

import jax
import jax.numpy as jnp
from jax import lax
from jax.experimental import pallas as pl
from jax.experimental.pallas import tpu as pltpu
from jax.sharding import PartitionSpec as P

STEPS = 4
WSHIFT = 2


time_step = 0.5


def from_offsets(value, axis, offsets):
    count, mine = (lax.axis_size(axis), lax.axis_index(axis))
    got = {}
    for k in offsets:
        if k in got:
            continue
        pairs = [(s, s - k) for s in range(count) if 0 <= s - k < count]
        if not pairs:
            got[k] = jnp.zeros_like(value)
            continue
        if -k in offsets and 2 * abs(k) >= count:
            pairs = pairs + [(s, s + k) for s in range(count) if 0 <= s + k < count]
            received = lax.ppermute(value, axis, pairs)
            for j in (k, -k):
                inside = jnp.logical_and(mine + j >= 0, mine + j < count)
                got[j] = jnp.where(inside, received, jnp.zeros_like(received))
            continue
        got[k] = lax.ppermute(value, axis, pairs)
    return got


def with_ring(cells, axis, dim, width, total):
    length = cells.shape[dim]
    head = lax.slice_in_dim(cells, 0, width, axis=dim)
    tail = lax.slice_in_dim(cells, length - width, length, axis=dim)
    if dim == cells.ndim - 1:
        def pack(values):
            return values.reshape(-1, width).T

        def unpack(values, shape):
            return values.T.reshape(shape)
    else:
        pack, unpack = (packed, unpacked)
    below = unpack(from_offsets(pack(tail), axis, (-1,))[-1], tail.shape)
    above = unpack(from_offsets(pack(head), axis, (1,))[1], head.shape)
    parts = [cells, above]
    gap = total - length - 2 * width
    if gap:
        gap_shape = list(cells.shape)
        gap_shape[dim] = gap
        parts.append(jnp.zeros(gap_shape, cells.dtype))
    parts.append(below)
    return jnp.concatenate(parts, axis=dim)


def ring_coordinates(start, length, width, total):
    marks = lax.broadcasted_iota(jnp.int32, (total,), 0)
    return jnp.where(
        marks < length + width,
        start + marks,
        jnp.where(marks >= total - width, start - (total - marks), -1),
    )


def packed(values):
    lanes = 128
    if values.size % lanes:
        return values.reshape(-1)
    return values.reshape(-1, lanes)


def unpacked(values, shape):
    return values.reshape(shape)


def upper_next(values, dimension):
    zeros_plane = jnp.zeros_like(lax.slice_in_dim(values, 0, 1, axis=dimension))
    rest = lax.slice_in_dim(values, 1, values.shape[dimension], axis=dimension)
    return jnp.concatenate([rest, zeros_plane], axis=dimension)


def lower_next(values, dimension):
    zeros_plane = jnp.zeros_like(lax.slice_in_dim(values, 0, 1, axis=dimension))
    rest = lax.slice_in_dim(values, 0, values.shape[dimension] - 1, axis=dimension)
    return jnp.concatenate([zeros_plane, rest], axis=dimension)


def forward_diff(values, dimension):
    return upper_next(values, dimension) - values


def backward_diff(values, dimension):
    return values - lower_next(values, dimension)


def curl_forward(field):
    field_x, field_y, field_z = field[0], field[1], field[2]
    return jnp.stack([forward_diff(field_z, 1) - forward_diff(field_y, 0),
                      forward_diff(field_x, 0) - forward_diff(field_z, 2),
                      forward_diff(field_y, 2) - forward_diff(field_x, 1)])


def curl_backward(field):
    field_x, field_y, field_z = field[0], field[1], field[2]
    return jnp.stack([backward_diff(field_z, 1) - backward_diff(field_y, 0),
                      backward_diff(field_x, 0) - backward_diff(field_z, 2),
                      backward_diff(field_y, 2) - backward_diff(field_x, 1)])


def advance_planes(values, amount, dimension):
    shape_pad = list(values.shape)
    shape_pad[dimension] = WSHIFT
    joined = jnp.concatenate([values, jnp.zeros(shape_pad, values.dtype)], axis=dimension)
    return lax.dynamic_slice_in_dim(joined, amount, values.shape[dimension], axis=dimension)


def cell_lookup(selector, table):
    return jnp.sum(jnp.where(selector, table[:, None, None], jnp.float32(0.0)), axis=0)


def inside_range(start, length, total, dimension, total_dims):
    shape_one = [1] * total_dims
    shape_one[dimension] = length
    marks = start + lax.broadcasted_iota(jnp.int32, tuple(shape_one), dimension)
    return jnp.logical_and(marks >= 0, marks < total)


def entering(value, axis):
    count, mine = (lax.axis_size(axis), lax.axis_index(axis))
    pieces = lax.all_gather(value, axis)
    running = jnp.zeros_like(value)
    for position in range(count - 1):
        running = jnp.where(position < mine, running + pieces[position], running)
    return running


def body(
    electric,
    magnetic,
    polarization,
    current,
    material,
    advance,
    permittivity,
    nonlinear,
    pole_strength,
    pole_frequency,
    pole_damping,
):
    planes, rows, columns = (electric.shape[1], electric.shape[2], electric.shape[3])
    n_prop, n_tx, n_ty = (lax.axis_size("prop"), lax.axis_size("tx"), lax.axis_size("ty"))
    total_z, total_y, total_x = (planes * n_prop, rows * n_ty, columns * n_tx)
    at_z, at_y, at_x = (lax.axis_index("prop"), lax.axis_index("ty"), lax.axis_index("tx"))
    halo = STEPS
    assert halo <= rows and halo <= columns

    state = jnp.concatenate(
        [
            electric,
            magnetic,
            polarization.reshape((-1,) + electric.shape[1:]),
            current.reshape((-1,) + electric.shape[1:]),
        ],
        axis=0,
    )

    below = -(-STEPS // planes)
    above = -(-(STEPS + STEPS * WSHIFT) // planes)
    whole_column = (below + above + 1) * planes >= total_z
    if whole_column:
        offsets = [k for k in range(-(n_prop - 1), n_prop) if k != 0]
        pieces = from_offsets(state, "prop", offsets)
        pieces[0] = state
        blocks = []
        for j in range(n_prop):
            block = jnp.zeros_like(state)
            for k, piece in pieces.items():
                block = jnp.where(at_z + k == j, piece, block)
            blocks.append(block)
        state = jnp.concatenate(blocks, axis=1)
        base_z = jnp.int32(0)
        own_z = at_z * planes
    else:
        offsets = [k for k in range(-below, above + 1) if k != 0]
        pieces = from_offsets(state, "prop", offsets)
        pieces[0] = state
        state = jnp.concatenate([pieces[k] for k in range(-below, above + 1)], axis=1)
        base_z = (at_z - below) * planes
        own_z = below * planes
    depth = state.shape[1]

    kinds = material.astype(jnp.float32)
    state = jnp.concatenate([state, jnp.broadcast_to(kinds[None, None], (1, depth, rows, columns))], axis=0)
    ring_rows = -(-(rows + 2 * halo) // 8) * 8
    ring_columns = -(-(columns + 2 * halo) // 128) * 128
    state = with_ring(state, "ty", 2, halo, ring_rows)
    state = with_ring(state, "tx", 3, halo, ring_columns)
    kinds = state[-1, 0].astype(jnp.int32)

    place_z = base_z + lax.broadcasted_iota(jnp.int32, (depth,), 0)
    place_y = ring_coordinates(at_y * rows, rows, halo, ring_rows)
    place_x = ring_coordinates(at_x * columns, columns, halo, ring_columns)
    keep_mask = (
        ((place_z >= 0) & (place_z < total_z))[:, None, None]
        & ((place_y >= 0) & (place_y < total_y))[None, :, None]
        & ((place_x >= 0) & (place_x < total_x))[None, None, :]
    ).astype(jnp.float32)

    materials_count = permittivity.shape[0]
    selector = kinds[None] == lax.broadcasted_iota(
        jnp.int32, (materials_count, ring_rows, ring_columns), 0
    )
    eps_cell = cell_lookup(selector, permittivity)
    kerr_cell = cell_lookup(selector, nonlinear)
    strength = [cell_lookup(selector, pole_strength[p]) for p in range(2)]
    frequency = [cell_lookup(selector, pole_frequency[p]) for p in range(2)]
    half_damp = [0.5 * time_step * cell_lookup(selector, pole_damping[p]) for p in range(2)]
    keep_rate = [(1.0 - h) / (1.0 + h) for h in half_damp]
    drive_rate = [time_step * f * f / (1.0 + h) for f, h in zip(frequency, half_damp)]
    coefficients = jnp.stack([eps_cell, kerr_cell] + strength + keep_rate + drive_rate)

    own_at = jnp.reshape(jnp.asarray(own_z, jnp.int32), (1,))
    fields = state.shape[0] - 1
    final, density = pl.pallas_call(
        functools.partial(steps_kernel, planes=planes, rows=rows, columns=columns),
        out_shape=(
            jax.ShapeDtypeStruct((fields, planes, rows, columns), jnp.float32),
            jax.ShapeDtypeStruct((depth, rows, columns), jnp.float32),
        ),
        in_specs=[
            pl.BlockSpec(memory_space=pltpu.SMEM),
            pl.BlockSpec(memory_space=pltpu.SMEM),
            pl.BlockSpec(memory_space=pltpu.VMEM),
            pl.BlockSpec(memory_space=pltpu.VMEM),
            pl.BlockSpec(memory_space=pltpu.VMEM),
        ],
        out_specs=(
            pl.BlockSpec(memory_space=pltpu.VMEM),
            pl.BlockSpec(memory_space=pltpu.VMEM),
        ),
        scratch_shapes=[pltpu.VMEM((fields, depth + WSHIFT, ring_rows, ring_columns), jnp.float32)],
    )(advance, own_at, state, coefficients, keep_mask)

    if whole_column:
        column_energy = lax.dynamic_slice_in_dim(jnp.cumsum(density, axis=0), own_z, planes, axis=0)
        column_energy = column_energy / jnp.float32(total_z)
    else:
        density = lax.slice_in_dim(density, own_z, own_z + planes, axis=0)
        prefix = entering(jnp.sum(density, axis=0), "prop")
        column_energy = (prefix[None] + jnp.cumsum(density, axis=0)) / jnp.float32(total_z)
    pole_shape = (2, 3) + final.shape[1:]
    return (
        final[0:3],
        final[3:6],
        final[6:12].reshape(pole_shape),
        final[12:18].reshape(pole_shape),
        column_energy,
    )


def steps_kernel(advance_ref, own_ref, state_ref, coef_ref, mask_ref, out_ref, density_ref, work_ref, *, planes, rows, columns):
    fields, depth = (work_ref.shape[0], work_ref.shape[1] - WSHIFT)
    work_ref[:, depth:] = jnp.zeros((fields, WSHIFT) + work_ref.shape[2:], jnp.float32)
    eps_cell, kerr_cell = (coef_ref[0], coef_ref[1])
    strength, keep_rate, drive_rate = (
        (coef_ref[2], coef_ref[3]),
        (coef_ref[4], coef_ref[5]),
        (coef_ref[6], coef_ref[7]),
    )
    keep_mask = mask_ref[...]
    zero_plane = jnp.zeros((1,) + keep_mask.shape[1:], jnp.float32)
    ring_rows, ring_columns = keep_mask.shape[1:]

    def up_z(f):
        return jnp.concatenate([f[1:], zero_plane], axis=0)

    def down_z(f):
        return jnp.concatenate([zero_plane, f[:-1]], axis=0)

    def up_y(f):
        return pltpu.roll(f, ring_rows - 1, 1)

    def down_y(f):
        return pltpu.roll(f, 1, 1)

    def up_x(f):
        return pltpu.roll(f, ring_columns - 1, 2)

    def down_x(f):
        return pltpu.roll(f, 1, 2)

    amount = None
    for moment in range(STEPS):
        if amount is None:
            values = [state_ref[c] for c in range(fields)]
        else:
            values = [work_ref[c, pl.ds(amount, depth)] for c in range(fields)]
        e_x, e_y, e_z = values[0:3]
        h_x, h_y, h_z = values[3:6]
        pol = [values[6:9], values[9:12]]
        cur = [values[12:15], values[15:18]]
        h_x = (h_x - time_step * ((up_y(e_z) - e_z) - (up_z(e_y) - e_y))) * keep_mask
        h_y = (h_y - time_step * ((up_z(e_x) - e_x) - (up_x(e_z) - e_z))) * keep_mask
        h_z = (h_z - time_step * ((up_x(e_y) - e_y) - (up_y(e_x) - e_x))) * keep_mask
        squared = e_x * e_x + e_y * e_y + e_z * e_z
        electric = (e_x, e_y, e_z)
        for p in range(2):
            for c in range(3):
                cur[p][c] = keep_rate[p] * cur[p][c] + drive_rate[p] * (strength[p] * electric[c] - pol[p][c])
                pol[p][c] = pol[p][c] + time_step * cur[p][c]
        curl_x = (h_z - down_y(h_z)) - (h_y - down_z(h_y))
        curl_y = (h_x - down_z(h_x)) - (h_z - down_x(h_z))
        curl_z = (h_y - down_x(h_y)) - (h_x - down_y(h_x))
        denominator = eps_cell + kerr_cell * squared
        new_e = [
            (field + time_step * (curl - cur[0][c] - cur[1][c]) / denominator) * keep_mask
            for c, (field, curl) in enumerate(zip(electric, (curl_x, curl_y, curl_z)))
        ]
        results = new_e + [h_x, h_y, h_z] + pol[0] + pol[1] + cur[0] + cur[1]
        for c in range(fields):
            work_ref[c, 0:depth] = results[c]
        amount = advance_ref[moment]

    start = amount + own_ref[0]
    for c in range(fields):
        out_ref[c] = work_ref[c, pl.ds(start, planes), 0:rows, 0:columns]
    squared_e = None
    squared_h = None
    for c in range(3):
        e = work_ref[c, pl.ds(amount, depth), 0:rows, 0:columns]
        h = work_ref[3 + c, pl.ds(amount, depth), 0:rows, 0:columns]
        squared_e = e * e if squared_e is None else squared_e + e * e
        squared_h = h * h if squared_h is None else squared_h + h * h
    density_ref[...] = eps_cell[0:rows, 0:columns][None] * squared_e + squared_h


def solution(mesh):
    return jax.shard_map(
        body,
        mesh=mesh,
        in_specs=(
            P(None, "prop", "ty", "tx"),
            P(None, "prop", "ty", "tx"),
            P(None, None, "prop", "ty", "tx"),
            P(None, None, "prop", "ty", "tx"),
            P("ty", "tx"),
            P(),
            P(),
            P(),
            P(),
            P(),
            P(),
        ),
        out_specs=(
            P(None, "prop", "ty", "tx"),
            P(None, "prop", "ty", "tx"),
            P(None, None, "prop", "ty", "tx"),
            P(None, None, "prop", "ty", "tx"),
            P("prop", "ty", "tx"),
        ),
        check_vma=False,
    )
```

```python
import functools

import jax
import jax.numpy as jnp
from jax import lax
from jax.experimental import pallas as pl
from jax.experimental.pallas import tpu as pltpu
from jax.sharding import PartitionSpec as P

STEPS = 4
WSHIFT = 2


time_step = 0.5


def from_offsets(value, axis, offsets):
    count, mine = (lax.axis_size(axis), lax.axis_index(axis))
    got = {}
    for k in offsets:
        if k in got:
            continue
        pairs = [(s, s - k) for s in range(count) if 0 <= s - k < count]
        if not pairs:
            got[k] = jnp.zeros_like(value)
            continue
        if -k in offsets and 2 * abs(k) >= count:
            pairs = pairs + [(s, s + k) for s in range(count) if 0 <= s + k < count]
            received = lax.ppermute(value, axis, pairs)
            for j in (k, -k):
                inside = jnp.logical_and(mine + j >= 0, mine + j < count)
                got[j] = jnp.where(inside, received, jnp.zeros_like(received))
            continue
        got[k] = lax.ppermute(value, axis, pairs)
    return got


def with_ring(cells, axis, dim, width, total):
    length = cells.shape[dim]
    head = lax.slice_in_dim(cells, 0, width, axis=dim)
    tail = lax.slice_in_dim(cells, length - width, length, axis=dim)
    if dim == cells.ndim - 1:
        def pack(values):
            return values.reshape(-1, width).T

        def unpack(values, shape):
            return values.T.reshape(shape)
    else:
        pack, unpack = (packed, unpacked)
    below = unpack(from_offsets(pack(tail), axis, (-1,))[-1], tail.shape)
    above = unpack(from_offsets(pack(head), axis, (1,))[1], head.shape)
    parts = [cells, above]
    gap = total - length - 2 * width
    if gap:
        gap_shape = list(cells.shape)
        gap_shape[dim] = gap
        parts.append(jnp.zeros(gap_shape, cells.dtype))
    parts.append(below)
    return jnp.concatenate(parts, axis=dim)


def ring_coordinates(start, length, width, total):
    marks = lax.broadcasted_iota(jnp.int32, (total,), 0)
    return jnp.where(
        marks < length + width,
        start + marks,
        jnp.where(marks >= total - width, start - (total - marks), -1),
    )


def packed(values):
    lanes = 128
    if values.size % lanes:
        return values.reshape(-1)
    return values.reshape(-1, lanes)


def unpacked(values, shape):
    return values.reshape(shape)


def upper_next(values, dimension):
    zeros_plane = jnp.zeros_like(lax.slice_in_dim(values, 0, 1, axis=dimension))
    rest = lax.slice_in_dim(values, 1, values.shape[dimension], axis=dimension)
    return jnp.concatenate([rest, zeros_plane], axis=dimension)


def lower_next(values, dimension):
    zeros_plane = jnp.zeros_like(lax.slice_in_dim(values, 0, 1, axis=dimension))
    rest = lax.slice_in_dim(values, 0, values.shape[dimension] - 1, axis=dimension)
    return jnp.concatenate([zeros_plane, rest], axis=dimension)


def forward_diff(values, dimension):
    return upper_next(values, dimension) - values


def backward_diff(values, dimension):
    return values - lower_next(values, dimension)


def curl_forward(field):
    field_x, field_y, field_z = field[0], field[1], field[2]
    return jnp.stack([forward_diff(field_z, 1) - forward_diff(field_y, 0),
                      forward_diff(field_x, 0) - forward_diff(field_z, 2),
                      forward_diff(field_y, 2) - forward_diff(field_x, 1)])


def curl_backward(field):
    field_x, field_y, field_z = field[0], field[1], field[2]
    return jnp.stack([backward_diff(field_z, 1) - backward_diff(field_y, 0),
                      backward_diff(field_x, 0) - backward_diff(field_z, 2),
                      backward_diff(field_y, 2) - backward_diff(field_x, 1)])


def advance_planes(values, amount, dimension):
    shape_pad = list(values.shape)
    shape_pad[dimension] = WSHIFT
    joined = jnp.concatenate([values, jnp.zeros(shape_pad, values.dtype)], axis=dimension)
    return lax.dynamic_slice_in_dim(joined, amount, values.shape[dimension], axis=dimension)


def cell_lookup(selector, table):
    return jnp.sum(jnp.where(selector, table[:, None, None], jnp.float32(0.0)), axis=0)


def inside_range(start, length, total, dimension, total_dims):
    shape_one = [1] * total_dims
    shape_one[dimension] = length
    marks = start + lax.broadcasted_iota(jnp.int32, tuple(shape_one), dimension)
    return jnp.logical_and(marks >= 0, marks < total)


def entering(value, axis):
    count, mine = (lax.axis_size(axis), lax.axis_index(axis))
    pieces = lax.all_gather(value, axis)
    running = jnp.zeros_like(value)
    for position in range(count - 1):
        running = jnp.where(position < mine, running + pieces[position], running)
    return running


def body(
    electric,
    magnetic,
    polarization,
    current,
    material,
    advance,
    permittivity,
    nonlinear,
    pole_strength,
    pole_frequency,
    pole_damping,
):
    planes, rows, columns = (electric.shape[1], electric.shape[2], electric.shape[3])
    n_prop, n_tx, n_ty = (lax.axis_size("prop"), lax.axis_size("tx"), lax.axis_size("ty"))
    total_z, total_y, total_x = (planes * n_prop, rows * n_ty, columns * n_tx)
    at_z, at_y, at_x = (lax.axis_index("prop"), lax.axis_index("ty"), lax.axis_index("tx"))
    halo = STEPS
    assert halo <= rows and halo <= columns

    state = jnp.concatenate(
        [
            electric,
            magnetic,
            polarization.reshape((-1,) + electric.shape[1:]),
            current.reshape((-1,) + electric.shape[1:]),
        ],
        axis=0,
    )

    below = -(-STEPS // planes)
    above = -(-(STEPS + STEPS * WSHIFT) // planes)
    whole_column = (below + above + 1) * planes >= total_z
    if whole_column:
        offsets = [k for k in range(-(n_prop - 1), n_prop) if k != 0]
        pieces = from_offsets(state, "prop", offsets)
        pieces[0] = state
        blocks = []
        for j in range(n_prop):
            block = jnp.zeros_like(state)
            for k, piece in pieces.items():
                block = jnp.where(at_z + k == j, piece, block)
            blocks.append(block)
        state = jnp.concatenate(blocks, axis=1)
        base_z = jnp.int32(0)
        own_z = at_z * planes
    else:
        offsets = [k for k in range(-below, above + 1) if k != 0]
        pieces = from_offsets(state, "prop", offsets)
        pieces[0] = state
        state = jnp.concatenate([pieces[k] for k in range(-below, above + 1)], axis=1)
        base_z = (at_z - below) * planes
        own_z = below * planes
    depth = state.shape[1]

    kinds = material.astype(jnp.float32)
    state = jnp.concatenate([state, jnp.broadcast_to(kinds[None, None], (1, depth, rows, columns))], axis=0)
    ring_rows = -(-(rows + 2 * halo) // 8) * 8
    ring_columns = -(-(columns + 2 * halo) // 128) * 128
    state = with_ring(state, "ty", 2, halo, ring_rows)
    state = with_ring(state, "tx", 3, halo, ring_columns)
    kinds = state[-1, 0].astype(jnp.int32)

    place_z = base_z + lax.broadcasted_iota(jnp.int32, (depth,), 0)
    place_y = ring_coordinates(at_y * rows, rows, halo, ring_rows)
    place_x = ring_coordinates(at_x * columns, columns, halo, ring_columns)
    keep_mask = (
        ((place_z >= 0) & (place_z < total_z))[:, None, None]
        & ((place_y >= 0) & (place_y < total_y))[None, :, None]
        & ((place_x >= 0) & (place_x < total_x))[None, None, :]
    ).astype(jnp.float32)

    materials_count = permittivity.shape[0]
    selector = kinds[None] == lax.broadcasted_iota(
        jnp.int32, (materials_count, ring_rows, ring_columns), 0
    )
    eps_cell = cell_lookup(selector, permittivity)
    kerr_cell = cell_lookup(selector, nonlinear)
    strength = [cell_lookup(selector, pole_strength[p]) for p in range(2)]
    frequency = [cell_lookup(selector, pole_frequency[p]) for p in range(2)]
    half_damp = [0.5 * time_step * cell_lookup(selector, pole_damping[p]) for p in range(2)]
    keep_rate = [(1.0 - h) / (1.0 + h) for h in half_damp]
    drive_rate = [time_step * f * f / (1.0 + h) for f, h in zip(frequency, half_damp)]
    coefficients = jnp.stack([eps_cell, kerr_cell] + strength + keep_rate + drive_rate)

    own_at = jnp.reshape(jnp.asarray(own_z, jnp.int32), (1,))
    fields = state.shape[0] - 1
    block = (planes, rows, columns)
    outs = pl.pallas_call(
        functools.partial(
            steps_kernel, planes=planes, rows=rows, columns=columns, whole=whole_column, total=total_z
        ),
        out_shape=(
            jax.ShapeDtypeStruct((3,) + block, jnp.float32),
            jax.ShapeDtypeStruct((3,) + block, jnp.float32),
            jax.ShapeDtypeStruct((2, 3) + block, jnp.float32),
            jax.ShapeDtypeStruct((2, 3) + block, jnp.float32),
            jax.ShapeDtypeStruct(block, jnp.float32),
        ),
        in_specs=[
            pl.BlockSpec(memory_space=pltpu.SMEM),
            pl.BlockSpec(memory_space=pltpu.SMEM),
            pl.BlockSpec(memory_space=pltpu.VMEM),
            pl.BlockSpec(memory_space=pltpu.VMEM),
            pl.BlockSpec(memory_space=pltpu.VMEM),
        ],
        out_specs=tuple(pl.BlockSpec(memory_space=pltpu.VMEM) for _ in range(5)),
        scratch_shapes=[
            pltpu.VMEM((fields, depth + WSHIFT, ring_rows, ring_columns), jnp.float32),
            pltpu.VMEM((depth, rows, columns), jnp.float32),
        ],
    )(advance, own_at, state, coefficients, keep_mask)
    electric_o, magnetic_o, polarization_o, current_o, column_energy = outs
    if not whole_column:
        prefix = entering(jnp.sum(column_energy, axis=0), "prop")
        column_energy = (prefix[None] + jnp.cumsum(column_energy, axis=0)) / jnp.float32(total_z)
    return (electric_o, magnetic_o, polarization_o, current_o, column_energy)


def steps_kernel(
    advance_ref, own_ref, state_ref, coef_ref, mask_ref,
    electric_ref, magnetic_ref, polarization_ref, current_ref, energy_ref,
    work_ref, running_ref, *, planes, rows, columns, whole, total,
):
    fields, depth = (work_ref.shape[0], work_ref.shape[1] - WSHIFT)
    work_ref[:, depth:] = jnp.zeros((fields, WSHIFT) + work_ref.shape[2:], jnp.float32)
    eps_cell, kerr_cell = (coef_ref[0], coef_ref[1])
    strength, keep_rate, drive_rate = (
        (coef_ref[2], coef_ref[3]),
        (coef_ref[4], coef_ref[5]),
        (coef_ref[6], coef_ref[7]),
    )
    keep_mask = mask_ref[...]
    zero_plane = jnp.zeros((1,) + keep_mask.shape[1:], jnp.float32)
    ring_rows, ring_columns = keep_mask.shape[1:]

    def up_z(f):
        return jnp.concatenate([f[1:], zero_plane], axis=0)

    def down_z(f):
        return jnp.concatenate([zero_plane, f[:-1]], axis=0)

    def up_y(f):
        return pltpu.roll(f, ring_rows - 1, 1)

    def down_y(f):
        return pltpu.roll(f, 1, 1)

    def up_x(f):
        return pltpu.roll(f, ring_columns - 1, 2)

    def down_x(f):
        return pltpu.roll(f, 1, 2)

    amount = None
    for moment in range(STEPS):
        if amount is None:
            values = [state_ref[c] for c in range(fields)]
        else:
            values = [work_ref[c, pl.ds(amount, depth)] for c in range(fields)]
        e_x, e_y, e_z = values[0:3]
        h_x, h_y, h_z = values[3:6]
        pol = [values[6:9], values[9:12]]
        cur = [values[12:15], values[15:18]]
        h_x = (h_x - time_step * ((up_y(e_z) - e_z) - (up_z(e_y) - e_y))) * keep_mask
        h_y = (h_y - time_step * ((up_z(e_x) - e_x) - (up_x(e_z) - e_z))) * keep_mask
        h_z = (h_z - time_step * ((up_x(e_y) - e_y) - (up_y(e_x) - e_x))) * keep_mask
        squared = e_x * e_x + e_y * e_y + e_z * e_z
        electric = (e_x, e_y, e_z)
        for p in range(2):
            for c in range(3):
                cur[p][c] = keep_rate[p] * cur[p][c] + drive_rate[p] * (strength[p] * electric[c] - pol[p][c])
                pol[p][c] = pol[p][c] + time_step * cur[p][c]
        curl_x = (h_z - down_y(h_z)) - (h_y - down_z(h_y))
        curl_y = (h_x - down_z(h_x)) - (h_z - down_x(h_z))
        curl_z = (h_y - down_x(h_y)) - (h_x - down_y(h_x))
        denominator = eps_cell + kerr_cell * squared
        new_e = [
            (field + time_step * (curl - cur[0][c] - cur[1][c]) / denominator) * keep_mask
            for c, (field, curl) in enumerate(zip(electric, (curl_x, curl_y, curl_z)))
        ]
        results = new_e + [h_x, h_y, h_z] + pol[0] + pol[1] + cur[0] + cur[1]
        for c in range(fields):
            work_ref[c, 0:depth] = results[c]
        amount = advance_ref[moment]

    start = amount + own_ref[0]
    for c in range(3):
        electric_ref[c] = work_ref[c, pl.ds(start, planes), 0:rows, 0:columns]
        magnetic_ref[c] = work_ref[3 + c, pl.ds(start, planes), 0:rows, 0:columns]
        for p in range(2):
            polarization_ref[p, c] = work_ref[6 + 3 * p + c, pl.ds(start, planes), 0:rows, 0:columns]
            current_ref[p, c] = work_ref[12 + 3 * p + c, pl.ds(start, planes), 0:rows, 0:columns]
    eps_own = eps_cell[0:rows, 0:columns]
    reach = depth if whole else planes
    first = amount if whole else start
    squared_e = None
    squared_h = None
    for c in range(3):
        e = work_ref[c, pl.ds(first, reach), 0:rows, 0:columns]
        h = work_ref[3 + c, pl.ds(first, reach), 0:rows, 0:columns]
        squared_e = e * e if squared_e is None else squared_e + e * e
        squared_h = h * h if squared_h is None else squared_h + h * h
    density = eps_own[None] * squared_e + squared_h
    if whole:
        total_so_far = density[0]
        running_ref[0] = total_so_far
        for z in range(1, depth):
            total_so_far = total_so_far + density[z]
            running_ref[z] = total_so_far
        energy_ref[...] = running_ref[pl.ds(own_ref[0], planes)] / jnp.float32(total)
    else:
        energy_ref[...] = density


def solution(mesh):
    return jax.shard_map(
        body,
        mesh=mesh,
        in_specs=(
            P(None, "prop", "ty", "tx"),
            P(None, "prop", "ty", "tx"),
            P(None, None, "prop", "ty", "tx"),
            P(None, None, "prop", "ty", "tx"),
            P("ty", "tx"),
            P(),
            P(),
            P(),
            P(),
            P(),
            P(),
        ),
        out_specs=(
            P(None, "prop", "ty", "tx"),
            P(None, "prop", "ty", "tx"),
            P(None, None, "prop", "ty", "tx"),
            P(None, None, "prop", "ty", "tx"),
            P("prop", "ty", "tx"),
        ),
        check_vma=False,
    )
```

```python
import functools

import jax
import jax.numpy as jnp
from jax import lax
from jax.experimental import pallas as pl
from jax.experimental.pallas import tpu as pltpu
from jax.sharding import PartitionSpec as P

STEPS = 4
WSHIFT = 2


time_step = 0.5


def from_offsets(value, axis, offsets):
    count, mine = (lax.axis_size(axis), lax.axis_index(axis))
    got = {}
    for k in offsets:
        if k in got:
            continue
        pairs = [(s, s - k) for s in range(count) if 0 <= s - k < count]
        if not pairs:
            got[k] = jnp.zeros_like(value)
            continue
        if -k in offsets and 2 * abs(k) >= count:
            pairs = pairs + [(s, s + k) for s in range(count) if 0 <= s + k < count]
            received = lax.ppermute(value, axis, pairs)
            for j in (k, -k):
                inside = jnp.logical_and(mine + j >= 0, mine + j < count)
                got[j] = jnp.where(inside, received, jnp.zeros_like(received))
            continue
        got[k] = lax.ppermute(value, axis, pairs)
    return got


def with_ring(cells, axis, dim, width, total):
    length = cells.shape[dim]
    head = lax.slice_in_dim(cells, 0, width, axis=dim)
    tail = lax.slice_in_dim(cells, length - width, length, axis=dim)
    if dim == cells.ndim - 1:
        def pack(values):
            return values.reshape(-1, width).T

        def unpack(values, shape):
            return values.T.reshape(shape)
    else:
        pack, unpack = (packed, unpacked)
    below = unpack(from_offsets(pack(tail), axis, (-1,))[-1], tail.shape)
    above = unpack(from_offsets(pack(head), axis, (1,))[1], head.shape)
    parts = [cells, above]
    gap = total - length - 2 * width
    if gap:
        gap_shape = list(cells.shape)
        gap_shape[dim] = gap
        parts.append(jnp.zeros(gap_shape, cells.dtype))
    parts.append(below)
    return jnp.concatenate(parts, axis=dim)


def ring_coordinates(start, length, width, total):
    marks = lax.broadcasted_iota(jnp.int32, (total,), 0)
    return jnp.where(
        marks < length + width,
        start + marks,
        jnp.where(marks >= total - width, start - (total - marks), -1),
    )


def packed(values):
    lanes = 128
    if values.size % lanes:
        return values.reshape(-1)
    return values.reshape(-1, lanes)


def unpacked(values, shape):
    return values.reshape(shape)


def upper_next(values, dimension):
    zeros_plane = jnp.zeros_like(lax.slice_in_dim(values, 0, 1, axis=dimension))
    rest = lax.slice_in_dim(values, 1, values.shape[dimension], axis=dimension)
    return jnp.concatenate([rest, zeros_plane], axis=dimension)


def lower_next(values, dimension):
    zeros_plane = jnp.zeros_like(lax.slice_in_dim(values, 0, 1, axis=dimension))
    rest = lax.slice_in_dim(values, 0, values.shape[dimension] - 1, axis=dimension)
    return jnp.concatenate([zeros_plane, rest], axis=dimension)


def forward_diff(values, dimension):
    return upper_next(values, dimension) - values


def backward_diff(values, dimension):
    return values - lower_next(values, dimension)


def curl_forward(field):
    field_x, field_y, field_z = field[0], field[1], field[2]
    return jnp.stack([forward_diff(field_z, 1) - forward_diff(field_y, 0),
                      forward_diff(field_x, 0) - forward_diff(field_z, 2),
                      forward_diff(field_y, 2) - forward_diff(field_x, 1)])


def curl_backward(field):
    field_x, field_y, field_z = field[0], field[1], field[2]
    return jnp.stack([backward_diff(field_z, 1) - backward_diff(field_y, 0),
                      backward_diff(field_x, 0) - backward_diff(field_z, 2),
                      backward_diff(field_y, 2) - backward_diff(field_x, 1)])


def advance_planes(values, amount, dimension):
    shape_pad = list(values.shape)
    shape_pad[dimension] = WSHIFT
    joined = jnp.concatenate([values, jnp.zeros(shape_pad, values.dtype)], axis=dimension)
    return lax.dynamic_slice_in_dim(joined, amount, values.shape[dimension], axis=dimension)


def cell_lookup(selector, table):
    return jnp.sum(jnp.where(selector, table[:, None, None], jnp.float32(0.0)), axis=0)


def inside_range(start, length, total, dimension, total_dims):
    shape_one = [1] * total_dims
    shape_one[dimension] = length
    marks = start + lax.broadcasted_iota(jnp.int32, tuple(shape_one), dimension)
    return jnp.logical_and(marks >= 0, marks < total)


def entering(value, axis):
    count, mine = (lax.axis_size(axis), lax.axis_index(axis))
    pieces = lax.all_gather(value, axis)
    running = jnp.zeros_like(value)
    for position in range(count - 1):
        running = jnp.where(position < mine, running + pieces[position], running)
    return running


def body(
    electric,
    magnetic,
    polarization,
    current,
    material,
    advance,
    permittivity,
    nonlinear,
    pole_strength,
    pole_frequency,
    pole_damping,
):
    planes, rows, columns = (electric.shape[1], electric.shape[2], electric.shape[3])
    n_prop, n_tx, n_ty = (lax.axis_size("prop"), lax.axis_size("tx"), lax.axis_size("ty"))
    total_z, total_y, total_x = (planes * n_prop, rows * n_ty, columns * n_tx)
    at_z, at_y, at_x = (lax.axis_index("prop"), lax.axis_index("ty"), lax.axis_index("tx"))
    halo = STEPS
    assert halo <= rows and halo <= columns

    state = jnp.concatenate(
        [
            electric,
            magnetic,
            polarization.reshape((-1,) + electric.shape[1:]),
            current.reshape((-1,) + electric.shape[1:]),
        ],
        axis=0,
    )

    below = -(-STEPS // planes)
    above = -(-(STEPS + STEPS * WSHIFT) // planes)
    whole_column = (below + above + 1) * planes >= total_z
    if whole_column:
        offsets = [k for k in range(-(n_prop - 1), n_prop) if k != 0]
        pieces = from_offsets(state, "prop", offsets)
        pieces[0] = state
        blocks = []
        for j in range(n_prop):
            block = jnp.zeros_like(state)
            for k, piece in pieces.items():
                block = jnp.where(at_z + k == j, piece, block)
            blocks.append(block)
        state = jnp.concatenate(blocks, axis=1)
        base_z = jnp.int32(0)
        own_z = at_z * planes
    else:
        offsets = [k for k in range(-below, above + 1) if k != 0]
        pieces = from_offsets(state, "prop", offsets)
        pieces[0] = state
        state = jnp.concatenate([pieces[k] for k in range(-below, above + 1)], axis=1)
        base_z = (at_z - below) * planes
        own_z = below * planes
    depth = state.shape[1]

    kinds = material.astype(jnp.float32)
    state = jnp.concatenate([state, jnp.broadcast_to(kinds[None, None], (1, depth, rows, columns))], axis=0)
    ring_rows = rows + 2 * halo
    tile = -(-2 * halo // 128) * 128
    ring_columns = columns + tile
    head = lax.slice_in_dim(state, 0, halo, axis=2)
    tail = lax.slice_in_dim(state, rows - halo, rows, axis=2)
    below = unpacked(from_offsets(packed(tail), "ty", (-1,))[-1], tail.shape)
    above = unpacked(from_offsets(packed(head), "ty", (1,))[1], head.shape)
    side = jnp.concatenate([above, below], axis=2)

    def columns_of(low, high):
        return jnp.concatenate(
            [lax.slice_in_dim(state, low, high, axis=3), lax.slice_in_dim(side, low, high, axis=3)], axis=2
        )

    x_head, x_tail = (columns_of(0, halo), columns_of(columns - halo, columns))
    from_right = from_offsets(x_head.reshape(-1, halo).T, "tx", (1,))[1]
    from_left = from_offsets(x_tail.reshape(-1, halo).T, "tx", (-1,))[-1]
    gap = jnp.zeros((tile - 2 * halo, from_right.shape[1]), jnp.float32)
    halo_tile = jnp.concatenate([from_right, gap, from_left], axis=0).T.reshape(x_head.shape[:-1] + (tile,))
    kinds = jnp.concatenate(
        [jnp.concatenate([state[-1, 0], side[-1, 0]], axis=0), halo_tile[-1, 0]], axis=1
    ).astype(jnp.int32)

    place_z = base_z + lax.broadcasted_iota(jnp.int32, (depth,), 0)
    place_y = ring_coordinates(at_y * rows, rows, halo, ring_rows)
    place_x = ring_coordinates(at_x * columns, columns, halo, ring_columns)
    keep_mask = (
        ((place_z >= 0) & (place_z < total_z))[:, None, None]
        & ((place_y >= 0) & (place_y < total_y))[None, :, None]
        & ((place_x >= 0) & (place_x < total_x))[None, None, :]
    ).astype(jnp.float32)

    materials_count = permittivity.shape[0]
    selector = kinds[None] == lax.broadcasted_iota(
        jnp.int32, (materials_count, ring_rows, ring_columns), 0
    )
    eps_cell = cell_lookup(selector, permittivity)
    kerr_cell = cell_lookup(selector, nonlinear)
    strength = [cell_lookup(selector, pole_strength[p]) for p in range(2)]
    frequency = [cell_lookup(selector, pole_frequency[p]) for p in range(2)]
    half_damp = [0.5 * time_step * cell_lookup(selector, pole_damping[p]) for p in range(2)]
    keep_rate = [(1.0 - h) / (1.0 + h) for h in half_damp]
    drive_rate = [time_step * f * f / (1.0 + h) for f, h in zip(frequency, half_damp)]
    coefficients = jnp.stack([eps_cell, kerr_cell] + strength + keep_rate + drive_rate)

    own_at = jnp.reshape(jnp.asarray(own_z, jnp.int32), (1,))
    fields = state.shape[0] - 1
    block = (planes, rows, columns)
    outs = pl.pallas_call(
        functools.partial(
            steps_kernel, planes=planes, rows=rows, columns=columns, whole=whole_column, total=total_z
        ),
        out_shape=(
            jax.ShapeDtypeStruct((3,) + block, jnp.float32),
            jax.ShapeDtypeStruct((3,) + block, jnp.float32),
            jax.ShapeDtypeStruct((2, 3) + block, jnp.float32),
            jax.ShapeDtypeStruct((2, 3) + block, jnp.float32),
            jax.ShapeDtypeStruct(block, jnp.float32),
        ),
        in_specs=[
            pl.BlockSpec(memory_space=pltpu.SMEM),
            pl.BlockSpec(memory_space=pltpu.SMEM),
        ]
        + [pl.BlockSpec(memory_space=pltpu.VMEM) for _ in range(5)],
        out_specs=tuple(pl.BlockSpec(memory_space=pltpu.VMEM) for _ in range(5)),
        scratch_shapes=[
            pltpu.VMEM((fields, depth + WSHIFT, ring_rows, ring_columns), jnp.float32),
            pltpu.VMEM((depth, rows, columns), jnp.float32),
        ],
    )(advance, own_at, state, side, halo_tile, coefficients, keep_mask)
    electric_o, magnetic_o, polarization_o, current_o, column_energy = outs
    if not whole_column:
        prefix = entering(jnp.sum(column_energy, axis=0), "prop")
        column_energy = (prefix[None] + jnp.cumsum(column_energy, axis=0)) / jnp.float32(total_z)
    return (electric_o, magnetic_o, polarization_o, current_o, column_energy)


def steps_kernel(
    advance_ref, own_ref, state_ref, side_ref, tile_ref, coef_ref, mask_ref,
    electric_ref, magnetic_ref, polarization_ref, current_ref, energy_ref,
    work_ref, running_ref, *, planes, rows, columns, whole, total,
):
    fields, depth = (work_ref.shape[0], work_ref.shape[1] - WSHIFT)
    work_ref[:, depth:] = jnp.zeros((fields, WSHIFT) + work_ref.shape[2:], jnp.float32)
    for c in range(fields):
        work_ref[c, 0:depth, 0:rows, 0:columns] = state_ref[c]
        work_ref[c, 0:depth, rows:, 0:columns] = side_ref[c]
        work_ref[c, 0:depth, :, columns:] = tile_ref[c]
    eps_cell, kerr_cell = (coef_ref[0], coef_ref[1])
    strength, keep_rate, drive_rate = (
        (coef_ref[2], coef_ref[3]),
        (coef_ref[4], coef_ref[5]),
        (coef_ref[6], coef_ref[7]),
    )
    keep_mask = mask_ref[...]
    zero_plane = jnp.zeros((1,) + keep_mask.shape[1:], jnp.float32)
    ring_rows, ring_columns = keep_mask.shape[1:]

    def up_z(f):
        return jnp.concatenate([f[1:], zero_plane], axis=0)

    def down_z(f):
        return jnp.concatenate([zero_plane, f[:-1]], axis=0)

    def up_y(f):
        return pltpu.roll(f, ring_rows - 1, 1)

    def down_y(f):
        return pltpu.roll(f, 1, 1)

    def up_x(f):
        return pltpu.roll(f, ring_columns - 1, 2)

    def down_x(f):
        return pltpu.roll(f, 1, 2)

    amount = 0
    for moment in range(STEPS):
        values = [work_ref[c, pl.ds(amount, depth)] for c in range(fields)]
        e_x, e_y, e_z = values[0:3]
        h_x, h_y, h_z = values[3:6]
        pol = [values[6:9], values[9:12]]
        cur = [values[12:15], values[15:18]]
        h_x = (h_x - time_step * ((up_y(e_z) - e_z) - (up_z(e_y) - e_y))) * keep_mask
        h_y = (h_y - time_step * ((up_z(e_x) - e_x) - (up_x(e_z) - e_z))) * keep_mask
        h_z = (h_z - time_step * ((up_x(e_y) - e_y) - (up_y(e_x) - e_x))) * keep_mask
        squared = e_x * e_x + e_y * e_y + e_z * e_z
        electric = (e_x, e_y, e_z)
        for p in range(2):
            for c in range(3):
                cur[p][c] = keep_rate[p] * cur[p][c] + drive_rate[p] * (strength[p] * electric[c] - pol[p][c])
                pol[p][c] = pol[p][c] + time_step * cur[p][c]
        curl_x = (h_z - down_y(h_z)) - (h_y - down_z(h_y))
        curl_y = (h_x - down_z(h_x)) - (h_z - down_x(h_z))
        curl_z = (h_y - down_x(h_y)) - (h_x - down_y(h_x))
        denominator = eps_cell + kerr_cell * squared
        new_e = [
            (field + time_step * (curl - cur[0][c] - cur[1][c]) / denominator) * keep_mask
            for c, (field, curl) in enumerate(zip(electric, (curl_x, curl_y, curl_z)))
        ]
        results = new_e + [h_x, h_y, h_z] + pol[0] + pol[1] + cur[0] + cur[1]
        for c in range(fields):
            work_ref[c, 0:depth] = results[c]
        amount = advance_ref[moment]

    start = amount + own_ref[0]
    for c in range(3):
        electric_ref[c] = work_ref[c, pl.ds(start, planes), 0:rows, 0:columns]
        magnetic_ref[c] = work_ref[3 + c, pl.ds(start, planes), 0:rows, 0:columns]
        for p in range(2):
            polarization_ref[p, c] = work_ref[6 + 3 * p + c, pl.ds(start, planes), 0:rows, 0:columns]
            current_ref[p, c] = work_ref[12 + 3 * p + c, pl.ds(start, planes), 0:rows, 0:columns]
    eps_own = eps_cell[0:rows, 0:columns]
    reach = depth if whole else planes
    first = amount if whole else start
    squared_e = None
    squared_h = None
    for c in range(3):
        e = work_ref[c, pl.ds(first, reach), 0:rows, 0:columns]
        h = work_ref[3 + c, pl.ds(first, reach), 0:rows, 0:columns]
        squared_e = e * e if squared_e is None else squared_e + e * e
        squared_h = h * h if squared_h is None else squared_h + h * h
    density = eps_own[None] * squared_e + squared_h
    if whole:
        total_so_far = density[0]
        running_ref[0] = total_so_far
        for z in range(1, depth):
            total_so_far = total_so_far + density[z]
            running_ref[z] = total_so_far
        energy_ref[...] = running_ref[pl.ds(own_ref[0], planes)] / jnp.float32(total)
    else:
        energy_ref[...] = density


def solution(mesh):
    return jax.shard_map(
        body,
        mesh=mesh,
        in_specs=(
            P(None, "prop", "ty", "tx"),
            P(None, "prop", "ty", "tx"),
            P(None, None, "prop", "ty", "tx"),
            P(None, None, "prop", "ty", "tx"),
            P("ty", "tx"),
            P(),
            P(),
            P(),
            P(),
            P(),
            P(),
        ),
        out_specs=(
            P(None, "prop", "ty", "tx"),
            P(None, "prop", "ty", "tx"),
            P(None, None, "prop", "ty", "tx"),
            P(None, None, "prop", "ty", "tx"),
            P("prop", "ty", "tx"),
        ),
        check_vma=False,
    )
```

```python
import functools

import jax
import jax.numpy as jnp
from jax import lax
from jax.experimental import pallas as pl
from jax.experimental.pallas import tpu as pltpu
from jax.sharding import PartitionSpec as P

STEPS = 4
WSHIFT = 2


time_step = 0.5


def from_offsets(value, axis, offsets):
    count, mine = (lax.axis_size(axis), lax.axis_index(axis))
    got = {}
    for k in offsets:
        if k in got:
            continue
        pairs = [(s, s - k) for s in range(count) if 0 <= s - k < count]
        if not pairs:
            got[k] = jnp.zeros_like(value)
            continue
        if -k in offsets and 2 * abs(k) >= count:
            pairs = pairs + [(s, s + k) for s in range(count) if 0 <= s + k < count]
            received = lax.ppermute(value, axis, pairs)
            for j in (k, -k):
                inside = jnp.logical_and(mine + j >= 0, mine + j < count)
                got[j] = jnp.where(inside, received, jnp.zeros_like(received))
            continue
        got[k] = lax.ppermute(value, axis, pairs)
    return got


def with_ring(cells, axis, dim, width, total):
    length = cells.shape[dim]
    head = lax.slice_in_dim(cells, 0, width, axis=dim)
    tail = lax.slice_in_dim(cells, length - width, length, axis=dim)
    if dim == cells.ndim - 1:
        def pack(values):
            return values.reshape(-1, width).T

        def unpack(values, shape):
            return values.T.reshape(shape)
    else:
        pack, unpack = (packed, unpacked)
    below = unpack(from_offsets(pack(tail), axis, (-1,))[-1], tail.shape)
    above = unpack(from_offsets(pack(head), axis, (1,))[1], head.shape)
    parts = [cells, above]
    gap = total - length - 2 * width
    if gap:
        gap_shape = list(cells.shape)
        gap_shape[dim] = gap
        parts.append(jnp.zeros(gap_shape, cells.dtype))
    parts.append(below)
    return jnp.concatenate(parts, axis=dim)


def ring_coordinates(start, length, width, total):
    marks = lax.broadcasted_iota(jnp.int32, (total,), 0)
    return jnp.where(
        marks < length + width,
        start + marks,
        jnp.where(marks >= total - width, start - (total - marks), -1),
    )


def packed(values):
    lanes = 128
    if values.size % lanes:
        return values.reshape(-1)
    return values.reshape(-1, lanes)


def unpacked(values, shape):
    return values.reshape(shape)


def upper_next(values, dimension):
    zeros_plane = jnp.zeros_like(lax.slice_in_dim(values, 0, 1, axis=dimension))
    rest = lax.slice_in_dim(values, 1, values.shape[dimension], axis=dimension)
    return jnp.concatenate([rest, zeros_plane], axis=dimension)


def lower_next(values, dimension):
    zeros_plane = jnp.zeros_like(lax.slice_in_dim(values, 0, 1, axis=dimension))
    rest = lax.slice_in_dim(values, 0, values.shape[dimension] - 1, axis=dimension)
    return jnp.concatenate([zeros_plane, rest], axis=dimension)


def forward_diff(values, dimension):
    return upper_next(values, dimension) - values


def backward_diff(values, dimension):
    return values - lower_next(values, dimension)


def curl_forward(field):
    field_x, field_y, field_z = field[0], field[1], field[2]
    return jnp.stack([forward_diff(field_z, 1) - forward_diff(field_y, 0),
                      forward_diff(field_x, 0) - forward_diff(field_z, 2),
                      forward_diff(field_y, 2) - forward_diff(field_x, 1)])


def curl_backward(field):
    field_x, field_y, field_z = field[0], field[1], field[2]
    return jnp.stack([backward_diff(field_z, 1) - backward_diff(field_y, 0),
                      backward_diff(field_x, 0) - backward_diff(field_z, 2),
                      backward_diff(field_y, 2) - backward_diff(field_x, 1)])


def advance_planes(values, amount, dimension):
    shape_pad = list(values.shape)
    shape_pad[dimension] = WSHIFT
    joined = jnp.concatenate([values, jnp.zeros(shape_pad, values.dtype)], axis=dimension)
    return lax.dynamic_slice_in_dim(joined, amount, values.shape[dimension], axis=dimension)


def cell_lookup(selector, table):
    return jnp.sum(jnp.where(selector, table[:, None, None], jnp.float32(0.0)), axis=0)


def inside_range(start, length, total, dimension, total_dims):
    shape_one = [1] * total_dims
    shape_one[dimension] = length
    marks = start + lax.broadcasted_iota(jnp.int32, tuple(shape_one), dimension)
    return jnp.logical_and(marks >= 0, marks < total)


def entering(value, axis):
    count, mine = (lax.axis_size(axis), lax.axis_index(axis))
    pieces = lax.all_gather(value, axis)
    running = jnp.zeros_like(value)
    for position in range(count - 1):
        running = jnp.where(position < mine, running + pieces[position], running)
    return running


def body(
    electric,
    magnetic,
    polarization,
    current,
    material,
    advance,
    permittivity,
    nonlinear,
    pole_strength,
    pole_frequency,
    pole_damping,
):
    planes, rows, columns = (electric.shape[1], electric.shape[2], electric.shape[3])
    n_prop, n_tx, n_ty = (lax.axis_size("prop"), lax.axis_size("tx"), lax.axis_size("ty"))
    total_z, total_y, total_x = (planes * n_prop, rows * n_ty, columns * n_tx)
    at_z, at_y, at_x = (lax.axis_index("prop"), lax.axis_index("ty"), lax.axis_index("tx"))
    halo = STEPS
    assert halo <= rows and halo <= columns

    state = jnp.concatenate(
        [
            electric,
            magnetic,
            polarization.reshape((-1,) + electric.shape[1:]),
            current.reshape((-1,) + electric.shape[1:]),
        ],
        axis=0,
    )

    below = -(-STEPS // planes)
    above = -(-(STEPS + STEPS * WSHIFT) // planes)
    whole_column = (below + above + 1) * planes >= total_z
    if whole_column:
        offsets = [k for k in range(-(n_prop - 1), n_prop) if k != 0]
        pieces = from_offsets(state, "prop", offsets)
        pieces[0] = state
        blocks = []
        for j in range(n_prop):
            block = jnp.zeros_like(state)
            for k, piece in pieces.items():
                block = jnp.where(at_z + k == j, piece, block)
            blocks.append(block)
        state = jnp.concatenate(blocks, axis=1)
        base_z = jnp.int32(0)
        own_z = at_z * planes
    else:
        offsets = [k for k in range(-below, above + 1) if k != 0]
        pieces = from_offsets(state, "prop", offsets)
        pieces[0] = state
        state = jnp.concatenate([pieces[k] for k in range(-below, above + 1)], axis=1)
        base_z = (at_z - below) * planes
        own_z = below * planes
    depth = state.shape[1]

    kinds = material.astype(jnp.float32)
    state = jnp.concatenate([state, jnp.broadcast_to(kinds[None, None], (1, depth, rows, columns))], axis=0)
    ring_rows = rows + 2 * halo
    tile = -(-2 * halo // 128) * 128
    ring_columns = columns + tile
    head = lax.slice_in_dim(state, 0, halo, axis=2)
    tail = lax.slice_in_dim(state, rows - halo, rows, axis=2)
    below = unpacked(from_offsets(packed(tail), "ty", (-1,))[-1], tail.shape)
    above = unpacked(from_offsets(packed(head), "ty", (1,))[1], head.shape)
    side = jnp.concatenate([above, below], axis=2)

    def columns_of(low, high):
        return jnp.concatenate(
            [lax.slice_in_dim(state, low, high, axis=3), lax.slice_in_dim(side, low, high, axis=3)], axis=2
        )

    x_head, x_tail = (columns_of(0, halo), columns_of(columns - halo, columns))
    strip_rows = -(-halo // 8) * 8
    strip_length = -(-x_head.size // halo // 128) * 128
    assert 2 * strip_rows <= tile

    def strip(values, at_top):
        flat = values.reshape(-1, halo).T
        room = strip_rows - halo
        rows_pad = (0, room) if at_top else (room, 0)
        return jnp.pad(flat, (rows_pad, (0, strip_length - flat.shape[1])))

    from_right = from_offsets(strip(x_head, True), "tx", (1,))[1]
    from_left = from_offsets(strip(x_tail, False), "tx", (-1,))[-1]

    place_z = base_z + lax.broadcasted_iota(jnp.int32, (depth,), 0)
    place_y = ring_coordinates(at_y * rows, rows, halo, ring_rows)
    place_x = ring_coordinates(at_x * columns, columns, halo, ring_columns)
    keep_mask = (
        ((place_z >= 0) & (place_z < total_z))[:, None, None]
        & ((place_y >= 0) & (place_y < total_y))[None, :, None]
        & ((place_x >= 0) & (place_x < total_x))[None, None, :]
    ).astype(jnp.float32)

    half_damp = 0.5 * time_step * pole_damping
    table = jnp.concatenate(
        [
            permittivity[None],
            nonlinear[None],
            pole_strength,
            (1.0 - half_damp) / (1.0 + half_damp),
            time_step * pole_frequency * pole_frequency / (1.0 + half_damp),
        ],
        axis=0,
    )

    own_at = jnp.reshape(jnp.asarray(own_z, jnp.int32), (1,))
    fields = state.shape[0]
    block = (planes, rows, columns)
    outs = pl.pallas_call(
        functools.partial(
            steps_kernel, planes=planes, rows=rows, columns=columns, whole=whole_column, total=total_z
        ),
        out_shape=(
            jax.ShapeDtypeStruct((3,) + block, jnp.float32),
            jax.ShapeDtypeStruct((3,) + block, jnp.float32),
            jax.ShapeDtypeStruct((2, 3) + block, jnp.float32),
            jax.ShapeDtypeStruct((2, 3) + block, jnp.float32),
            jax.ShapeDtypeStruct(block, jnp.float32),
        ),
        in_specs=[
            pl.BlockSpec(memory_space=pltpu.SMEM),
            pl.BlockSpec(memory_space=pltpu.SMEM),
            pl.BlockSpec(memory_space=pltpu.SMEM),
        ]
        + [pl.BlockSpec(memory_space=pltpu.VMEM) for _ in range(5)],
        out_specs=tuple(pl.BlockSpec(memory_space=pltpu.VMEM) for _ in range(5)),
        scratch_shapes=[
            pltpu.VMEM((fields, depth + WSHIFT, ring_rows, ring_columns), jnp.float32),
            pltpu.VMEM((depth, rows, columns), jnp.float32),
            pltpu.VMEM((tile, strip_length), jnp.float32),
            pltpu.VMEM((strip_length, tile), jnp.float32),
        ],
    )(advance, own_at, table, state, side, from_right, from_left, keep_mask)
    electric_o, magnetic_o, polarization_o, current_o, column_energy = outs
    if not whole_column:
        prefix = entering(jnp.sum(column_energy, axis=0), "prop")
        column_energy = (prefix[None] + jnp.cumsum(column_energy, axis=0)) / jnp.float32(total_z)
    return (electric_o, magnetic_o, polarization_o, current_o, column_energy)


def steps_kernel(
    advance_ref, own_ref, table_ref, state_ref, side_ref, right_ref, left_ref, mask_ref,
    electric_ref, magnetic_ref, polarization_ref, current_ref, energy_ref,
    work_ref, running_ref, strips_ref, turned_ref, *, planes, rows, columns, whole, total,
):
    fields, depth = (work_ref.shape[0], work_ref.shape[1] - WSHIFT)
    ring_rows = work_ref.shape[2]
    tile = strips_ref.shape[0]
    strip_rows = right_ref.shape[0]
    work_ref[:, depth:] = jnp.zeros((fields, WSHIFT) + work_ref.shape[2:], jnp.float32)
    strips_ref[...] = jnp.zeros(strips_ref.shape, jnp.float32)
    strips_ref[0:strip_rows] = right_ref[...]
    strips_ref[tile - strip_rows:tile] = left_ref[...]
    turned_ref[...] = strips_ref[...].T
    for c in range(fields):
        work_ref[c, 0:depth, 0:rows, 0:columns] = state_ref[c]
        work_ref[c, 0:depth, rows:, 0:columns] = side_ref[c]
        for z in range(depth):
            first_row = (c * depth + z) * ring_rows
            work_ref[c, z, :, columns:] = turned_ref[first_row:first_row + ring_rows]
    kinds = work_ref[fields - 1, 0]

    def lookup(row):
        cell = jnp.zeros(kinds.shape, jnp.float32)
        for m in range(table_ref.shape[1]):
            cell = jnp.where(kinds == jnp.float32(m), table_ref[row, m], cell)
        return cell

    eps_cell, kerr_cell = (lookup(0), lookup(1))
    strength, keep_rate, drive_rate = ((lookup(2), lookup(3)), (lookup(4), lookup(5)), (lookup(6), lookup(7)))
    keep_mask = mask_ref[...]
    zero_plane = jnp.zeros((1,) + keep_mask.shape[1:], jnp.float32)
    ring_rows, ring_columns = keep_mask.shape[1:]

    def up_z(f):
        return jnp.concatenate([f[1:], zero_plane], axis=0)

    def down_z(f):
        return jnp.concatenate([zero_plane, f[:-1]], axis=0)

    def up_y(f):
        return pltpu.roll(f, ring_rows - 1, 1)

    def down_y(f):
        return pltpu.roll(f, 1, 1)

    def up_x(f):
        return pltpu.roll(f, ring_columns - 1, 2)

    def down_x(f):
        return pltpu.roll(f, 1, 2)

    amount = 0
    for moment in range(STEPS):
        values = [work_ref[c, pl.ds(amount, depth)] for c in range(fields - 1)]
        e_x, e_y, e_z = values[0:3]
        h_x, h_y, h_z = values[3:6]
        pol = [values[6:9], values[9:12]]
        cur = [values[12:15], values[15:18]]
        h_x = (h_x - time_step * ((up_y(e_z) - e_z) - (up_z(e_y) - e_y))) * keep_mask
        h_y = (h_y - time_step * ((up_z(e_x) - e_x) - (up_x(e_z) - e_z))) * keep_mask
        h_z = (h_z - time_step * ((up_x(e_y) - e_y) - (up_y(e_x) - e_x))) * keep_mask
        squared = e_x * e_x + e_y * e_y + e_z * e_z
        electric = (e_x, e_y, e_z)
        for p in range(2):
            for c in range(3):
                cur[p][c] = keep_rate[p] * cur[p][c] + drive_rate[p] * (strength[p] * electric[c] - pol[p][c])
                pol[p][c] = pol[p][c] + time_step * cur[p][c]
        curl_x = (h_z - down_y(h_z)) - (h_y - down_z(h_y))
        curl_y = (h_x - down_z(h_x)) - (h_z - down_x(h_z))
        curl_z = (h_y - down_x(h_y)) - (h_x - down_y(h_x))
        denominator = eps_cell + kerr_cell * squared
        new_e = [
            (field + time_step * (curl - cur[0][c] - cur[1][c]) / denominator) * keep_mask
            for c, (field, curl) in enumerate(zip(electric, (curl_x, curl_y, curl_z)))
        ]
        results = new_e + [h_x, h_y, h_z] + pol[0] + pol[1] + cur[0] + cur[1]
        for c in range(fields - 1):
            work_ref[c, 0:depth] = results[c]
        amount = advance_ref[moment]

    start = amount + own_ref[0]
    for c in range(3):
        electric_ref[c] = work_ref[c, pl.ds(start, planes), 0:rows, 0:columns]
        magnetic_ref[c] = work_ref[3 + c, pl.ds(start, planes), 0:rows, 0:columns]
        for p in range(2):
            polarization_ref[p, c] = work_ref[6 + 3 * p + c, pl.ds(start, planes), 0:rows, 0:columns]
            current_ref[p, c] = work_ref[12 + 3 * p + c, pl.ds(start, planes), 0:rows, 0:columns]
    eps_own = eps_cell[0:rows, 0:columns]
    reach = depth if whole else planes
    first = amount if whole else start
    squared_e = None
    squared_h = None
    for c in range(3):
        e = work_ref[c, pl.ds(first, reach), 0:rows, 0:columns]
        h = work_ref[3 + c, pl.ds(first, reach), 0:rows, 0:columns]
        squared_e = e * e if squared_e is None else squared_e + e * e
        squared_h = h * h if squared_h is None else squared_h + h * h
    density = eps_own[None] * squared_e + squared_h
    if whole:
        total_so_far = density[0]
        running_ref[0] = total_so_far
        for z in range(1, depth):
            total_so_far = total_so_far + density[z]
            running_ref[z] = total_so_far
        energy_ref[...] = running_ref[pl.ds(own_ref[0], planes)] / jnp.float32(total)
    else:
        energy_ref[...] = density


def solution(mesh):
    return jax.shard_map(
        body,
        mesh=mesh,
        in_specs=(
            P(None, "prop", "ty", "tx"),
            P(None, "prop", "ty", "tx"),
            P(None, None, "prop", "ty", "tx"),
            P(None, None, "prop", "ty", "tx"),
            P("ty", "tx"),
            P(),
            P(),
            P(),
            P(),
            P(),
            P(),
        ),
        out_specs=(
            P(None, "prop", "ty", "tx"),
            P(None, "prop", "ty", "tx"),
            P(None, None, "prop", "ty", "tx"),
            P(None, None, "prop", "ty", "tx"),
            P("prop", "ty", "tx"),
        ),
        check_vma=False,
    )
```

```python
import functools

import jax
import jax.numpy as jnp
from jax import lax
from jax.experimental import pallas as pl
from jax.experimental.pallas import tpu as pltpu
from jax.sharding import PartitionSpec as P

STEPS = 4
WSHIFT = 2


time_step = 0.5


def from_offsets(value, axis, offsets):
    count, mine = (lax.axis_size(axis), lax.axis_index(axis))
    got = {}
    for k in offsets:
        if k in got:
            continue
        pairs = [(s, s - k) for s in range(count) if 0 <= s - k < count]
        if not pairs:
            got[k] = jnp.zeros_like(value)
            continue
        if -k in offsets and 2 * abs(k) >= count:
            pairs = pairs + [(s, s + k) for s in range(count) if 0 <= s + k < count]
            received = lax.ppermute(value, axis, pairs)
            for j in (k, -k):
                inside = jnp.logical_and(mine + j >= 0, mine + j < count)
                got[j] = jnp.where(inside, received, jnp.zeros_like(received))
            continue
        got[k] = lax.ppermute(value, axis, pairs)
    return got


def with_ring(cells, axis, dim, width, total):
    length = cells.shape[dim]
    head = lax.slice_in_dim(cells, 0, width, axis=dim)
    tail = lax.slice_in_dim(cells, length - width, length, axis=dim)
    if dim == cells.ndim - 1:
        def pack(values):
            return values.reshape(-1, width).T

        def unpack(values, shape):
            return values.T.reshape(shape)
    else:
        pack, unpack = (packed, unpacked)
    below = unpack(from_offsets(pack(tail), axis, (-1,))[-1], tail.shape)
    above = unpack(from_offsets(pack(head), axis, (1,))[1], head.shape)
    parts = [cells, above]
    gap = total - length - 2 * width
    if gap:
        gap_shape = list(cells.shape)
        gap_shape[dim] = gap
        parts.append(jnp.zeros(gap_shape, cells.dtype))
    parts.append(below)
    return jnp.concatenate(parts, axis=dim)


def ring_coordinates(start, length, width, total):
    marks = lax.broadcasted_iota(jnp.int32, (total,), 0)
    return jnp.where(
        marks < length + width,
        start + marks,
        jnp.where(marks >= total - width, start - (total - marks), -1),
    )


def packed(values):
    lanes = 128
    if values.size % lanes:
        return values.reshape(-1)
    return values.reshape(-1, lanes)


def unpacked(values, shape):
    return values.reshape(shape)


def upper_next(values, dimension):
    zeros_plane = jnp.zeros_like(lax.slice_in_dim(values, 0, 1, axis=dimension))
    rest = lax.slice_in_dim(values, 1, values.shape[dimension], axis=dimension)
    return jnp.concatenate([rest, zeros_plane], axis=dimension)


def lower_next(values, dimension):
    zeros_plane = jnp.zeros_like(lax.slice_in_dim(values, 0, 1, axis=dimension))
    rest = lax.slice_in_dim(values, 0, values.shape[dimension] - 1, axis=dimension)
    return jnp.concatenate([zeros_plane, rest], axis=dimension)


def forward_diff(values, dimension):
    return upper_next(values, dimension) - values


def backward_diff(values, dimension):
    return values - lower_next(values, dimension)


def curl_forward(field):
    field_x, field_y, field_z = field[0], field[1], field[2]
    return jnp.stack([forward_diff(field_z, 1) - forward_diff(field_y, 0),
                      forward_diff(field_x, 0) - forward_diff(field_z, 2),
                      forward_diff(field_y, 2) - forward_diff(field_x, 1)])


def curl_backward(field):
    field_x, field_y, field_z = field[0], field[1], field[2]
    return jnp.stack([backward_diff(field_z, 1) - backward_diff(field_y, 0),
                      backward_diff(field_x, 0) - backward_diff(field_z, 2),
                      backward_diff(field_y, 2) - backward_diff(field_x, 1)])


def advance_planes(values, amount, dimension):
    shape_pad = list(values.shape)
    shape_pad[dimension] = WSHIFT
    joined = jnp.concatenate([values, jnp.zeros(shape_pad, values.dtype)], axis=dimension)
    return lax.dynamic_slice_in_dim(joined, amount, values.shape[dimension], axis=dimension)


def cell_lookup(selector, table):
    return jnp.sum(jnp.where(selector, table[:, None, None], jnp.float32(0.0)), axis=0)


def inside_range(start, length, total, dimension, total_dims):
    shape_one = [1] * total_dims
    shape_one[dimension] = length
    marks = start + lax.broadcasted_iota(jnp.int32, tuple(shape_one), dimension)
    return jnp.logical_and(marks >= 0, marks < total)


def entering(value, axis):
    count, mine = (lax.axis_size(axis), lax.axis_index(axis))
    pieces = lax.all_gather(value, axis)
    running = jnp.zeros_like(value)
    for position in range(count - 1):
        running = jnp.where(position < mine, running + pieces[position], running)
    return running


def body(
    electric,
    magnetic,
    polarization,
    current,
    material,
    advance,
    permittivity,
    nonlinear,
    pole_strength,
    pole_frequency,
    pole_damping,
):
    planes, rows, columns = (electric.shape[1], electric.shape[2], electric.shape[3])
    n_prop, n_tx, n_ty = (lax.axis_size("prop"), lax.axis_size("tx"), lax.axis_size("ty"))
    total_z, total_y, total_x = (planes * n_prop, rows * n_ty, columns * n_tx)
    at_z, at_y, at_x = (lax.axis_index("prop"), lax.axis_index("ty"), lax.axis_index("tx"))
    halo = STEPS
    assert halo <= rows and halo <= columns

    state = jnp.concatenate(
        [
            electric,
            magnetic,
            polarization.reshape((-1,) + electric.shape[1:]),
            current.reshape((-1,) + electric.shape[1:]),
        ],
        axis=0,
    )

    below = -(-STEPS // planes)
    above = -(-(STEPS + STEPS * WSHIFT) // planes)
    whole_column = (below + above + 1) * planes >= total_z
    if whole_column:
        offsets = [k for k in range(-(n_prop - 1), n_prop) if k != 0]
        pieces = from_offsets(state, "prop", offsets)
        pieces[0] = state
        blocks = []
        for j in range(n_prop):
            block = jnp.zeros_like(state)
            for k, piece in pieces.items():
                block = jnp.where(at_z + k == j, piece, block)
            blocks.append(block)
        state = jnp.concatenate(blocks, axis=1)
        base_z = jnp.int32(0)
        own_z = at_z * planes
    else:
        offsets = [k for k in range(-below, above + 1) if k != 0]
        pieces = from_offsets(state, "prop", offsets)
        pieces[0] = state
        state = jnp.concatenate([pieces[k] for k in range(-below, above + 1)], axis=1)
        base_z = (at_z - below) * planes
        own_z = below * planes
    depth = state.shape[1]

    kinds = material.astype(jnp.float32)
    state = jnp.concatenate([state, jnp.broadcast_to(kinds[None, None], (1, depth, rows, columns))], axis=0)
    ring_rows = rows + 2 * halo
    tile = -(-2 * halo // 128) * 128
    ring_columns = columns + tile
    head = lax.slice_in_dim(state, 0, halo, axis=2)
    tail = lax.slice_in_dim(state, rows - halo, rows, axis=2)
    below = unpacked(from_offsets(packed(tail), "ty", (-1,))[-1], tail.shape)
    above = unpacked(from_offsets(packed(head), "ty", (1,))[1], head.shape)
    side = jnp.concatenate([above, below], axis=2)

    def columns_of(low, high):
        return jnp.concatenate(
            [lax.slice_in_dim(state, low, high, axis=3), lax.slice_in_dim(side, low, high, axis=3)], axis=2
        )

    x_head, x_tail = (columns_of(0, halo), columns_of(columns - halo, columns))
    strip_rows = -(-halo // 8) * 8
    strip_length = -(-x_head.size // halo // 128) * 128
    assert 2 * strip_rows <= tile

    def strip(values, at_top):
        flat = values.reshape(-1, halo).T
        room = strip_rows - halo
        rows_pad = (0, room) if at_top else (room, 0)
        return jnp.pad(flat, (rows_pad, (0, strip_length - flat.shape[1])))

    from_right = from_offsets(strip(x_head, True), "tx", (1,))[1]
    from_left = from_offsets(strip(x_tail, False), "tx", (-1,))[-1]

    place_z = base_z + lax.broadcasted_iota(jnp.int32, (depth,), 0)
    place_y = ring_coordinates(at_y * rows, rows, halo, ring_rows)
    place_x = ring_coordinates(at_x * columns, columns, halo, ring_columns)
    keep_mask = (
        ((place_z >= 0) & (place_z < total_z))[:, None, None]
        & ((place_y >= 0) & (place_y < total_y))[None, :, None]
        & ((place_x >= 0) & (place_x < total_x))[None, None, :]
    ).astype(jnp.float32)

    half_damp = 0.5 * time_step * pole_damping
    table = jnp.concatenate(
        [
            permittivity[None],
            nonlinear[None],
            pole_strength,
            (1.0 - half_damp) / (1.0 + half_damp),
            time_step * pole_frequency * pole_frequency / (1.0 + half_damp),
        ],
        axis=0,
    )

    own_at = jnp.reshape(jnp.asarray(own_z, jnp.int32), (1,))
    fields = state.shape[0]
    block = (planes, rows, columns)
    outs = pl.pallas_call(
        functools.partial(
            steps_kernel, planes=planes, rows=rows, columns=columns, whole=whole_column, total=total_z
        ),
        out_shape=(
            jax.ShapeDtypeStruct((3,) + block, jnp.float32),
            jax.ShapeDtypeStruct((3,) + block, jnp.float32),
            jax.ShapeDtypeStruct((2, 3) + block, jnp.float32),
            jax.ShapeDtypeStruct((2, 3) + block, jnp.float32),
            jax.ShapeDtypeStruct(block, jnp.float32),
        ),
        in_specs=[
            pl.BlockSpec(memory_space=pltpu.SMEM),
            pl.BlockSpec(memory_space=pltpu.SMEM),
            pl.BlockSpec(memory_space=pltpu.SMEM),
        ]
        + [pl.BlockSpec(memory_space=pltpu.VMEM) for _ in range(5)],
        out_specs=tuple(pl.BlockSpec(memory_space=pltpu.VMEM) for _ in range(5)),
        scratch_shapes=[
            pltpu.VMEM((fields, depth + WSHIFT, ring_rows, ring_columns), jnp.float32),
            pltpu.VMEM((depth, rows, columns), jnp.float32),
            pltpu.VMEM((tile, strip_length), jnp.float32),
            pltpu.VMEM((strip_length, tile), jnp.float32),
        ],
    )(advance, own_at, table, state, side, from_right, from_left, keep_mask)
    electric_o, magnetic_o, polarization_o, current_o, column_energy = outs
    if not whole_column:
        prefix = entering(jnp.sum(column_energy, axis=0), "prop")
        column_energy = (prefix[None] + jnp.cumsum(column_energy, axis=0)) / jnp.float32(total_z)
    return (electric_o, magnetic_o, polarization_o, current_o, column_energy)


def steps_kernel(
    advance_ref, own_ref, table_ref, state_ref, side_ref, right_ref, left_ref, mask_ref,
    electric_ref, magnetic_ref, polarization_ref, current_ref, energy_ref,
    work_ref, running_ref, strips_ref, turned_ref, *, planes, rows, columns, whole, total,
):
    fields, depth = (work_ref.shape[0], work_ref.shape[1] - WSHIFT)
    ring_rows = work_ref.shape[2]
    tile = strips_ref.shape[0]
    strip_rows = right_ref.shape[0]
    work_ref[:, depth:] = jnp.zeros((fields, WSHIFT) + work_ref.shape[2:], jnp.float32)
    strips_ref[...] = jnp.zeros(strips_ref.shape, jnp.float32)
    strips_ref[0:strip_rows] = right_ref[...]
    strips_ref[tile - strip_rows:tile] = left_ref[...]
    turned_ref[...] = strips_ref[...].T
    for c in range(fields):
        work_ref[c, 0:depth, 0:rows, 0:columns] = state_ref[c]
        work_ref[c, 0:depth, rows:, 0:columns] = side_ref[c]
        for z in range(depth):
            first_row = (c * depth + z) * ring_rows
            work_ref[c, z, :, columns:] = turned_ref[first_row:first_row + ring_rows]
    kinds = work_ref[fields - 1, 0]

    def lookup(row):
        cell = jnp.zeros(kinds.shape, jnp.float32)
        for m in range(table_ref.shape[1]):
            cell = jnp.where(kinds == jnp.float32(m), table_ref[row, m], cell)
        return cell

    eps_cell, kerr_cell = (lookup(0), lookup(1))
    strength, keep_rate, drive_rate = ((lookup(2), lookup(3)), (lookup(4), lookup(5)), (lookup(6), lookup(7)))
    keep_mask = mask_ref[...]
    zero_plane = jnp.zeros((1,) + keep_mask.shape[1:], jnp.float32)
    ring_rows, ring_columns = keep_mask.shape[1:]

    def up_z(f):
        return jnp.concatenate([f[1:], zero_plane], axis=0)

    def down_z(f):
        return jnp.concatenate([zero_plane, f[:-1]], axis=0)

    def up_y(f):
        return pltpu.roll(f, ring_rows - 1, 1)

    def down_y(f):
        return pltpu.roll(f, 1, 1)

    def up_x(f):
        return pltpu.roll(f, ring_columns - 1, 2)

    def down_x(f):
        return pltpu.roll(f, 1, 2)

    amount = 0
    for moment in range(STEPS):
        values = [work_ref[c, pl.ds(amount, depth)] for c in range(fields - 1)]
        e_x, e_y, e_z = values[0:3]
        h_x, h_y, h_z = values[3:6]
        pol = [values[6:9], values[9:12]]
        cur = [values[12:15], values[15:18]]
        h_x = (h_x - time_step * ((up_y(e_z) - e_z) - (up_z(e_y) - e_y))) * keep_mask
        h_y = (h_y - time_step * ((up_z(e_x) - e_x) - (up_x(e_z) - e_z))) * keep_mask
        h_z = (h_z - time_step * ((up_x(e_y) - e_y) - (up_y(e_x) - e_x))) * keep_mask
        squared = e_x * e_x + e_y * e_y + e_z * e_z
        electric = (e_x, e_y, e_z)
        for p in range(2):
            for c in range(3):
                cur[p][c] = keep_rate[p] * cur[p][c] + drive_rate[p] * (strength[p] * electric[c] - pol[p][c])
                pol[p][c] = pol[p][c] + time_step * cur[p][c]
        curl_x = (h_z - down_y(h_z)) - (h_y - down_z(h_y))
        curl_y = (h_x - down_z(h_x)) - (h_z - down_x(h_z))
        curl_z = (h_y - down_x(h_y)) - (h_x - down_y(h_x))
        inverse = 1.0 / (eps_cell + kerr_cell * squared)
        new_e = [
            (field + time_step * (curl - cur[0][c] - cur[1][c]) * inverse) * keep_mask
            for c, (field, curl) in enumerate(zip(electric, (curl_x, curl_y, curl_z)))
        ]
        results = new_e + [h_x, h_y, h_z] + pol[0] + pol[1] + cur[0] + cur[1]
        for c in range(fields - 1):
            work_ref[c, 0:depth] = results[c]
        amount = advance_ref[moment]

    start = amount + own_ref[0]
    for c in range(3):
        electric_ref[c] = work_ref[c, pl.ds(start, planes), 0:rows, 0:columns]
        magnetic_ref[c] = work_ref[3 + c, pl.ds(start, planes), 0:rows, 0:columns]
        for p in range(2):
            polarization_ref[p, c] = work_ref[6 + 3 * p + c, pl.ds(start, planes), 0:rows, 0:columns]
            current_ref[p, c] = work_ref[12 + 3 * p + c, pl.ds(start, planes), 0:rows, 0:columns]
    eps_own = eps_cell[0:rows, 0:columns]
    reach = depth if whole else planes
    first = amount if whole else start
    squared_e = None
    squared_h = None
    for c in range(3):
        e = work_ref[c, pl.ds(first, reach), 0:rows, 0:columns]
        h = work_ref[3 + c, pl.ds(first, reach), 0:rows, 0:columns]
        squared_e = e * e if squared_e is None else squared_e + e * e
        squared_h = h * h if squared_h is None else squared_h + h * h
    density = eps_own[None] * squared_e + squared_h
    if whole:
        total_so_far = density[0]
        running_ref[0] = total_so_far
        for z in range(1, depth):
            total_so_far = total_so_far + density[z]
            running_ref[z] = total_so_far
        energy_ref[...] = running_ref[pl.ds(own_ref[0], planes)] / jnp.float32(total)
    else:
        energy_ref[...] = density


def solution(mesh):
    return jax.shard_map(
        body,
        mesh=mesh,
        in_specs=(
            P(None, "prop", "ty", "tx"),
            P(None, "prop", "ty", "tx"),
            P(None, None, "prop", "ty", "tx"),
            P(None, None, "prop", "ty", "tx"),
            P("ty", "tx"),
            P(),
            P(),
            P(),
            P(),
            P(),
            P(),
        ),
        out_specs=(
            P(None, "prop", "ty", "tx"),
            P(None, "prop", "ty", "tx"),
            P(None, None, "prop", "ty", "tx"),
            P(None, None, "prop", "ty", "tx"),
            P("prop", "ty", "tx"),
        ),
        check_vma=False,
    )
```

```python
import functools

import jax
import jax.numpy as jnp
from jax import lax
from jax.experimental import pallas as pl
from jax.experimental.pallas import tpu as pltpu
from jax.sharding import PartitionSpec as P

STEPS = 4
WSHIFT = 2


time_step = 0.5


def from_offsets(value, axis, offsets):
    count, mine = (lax.axis_size(axis), lax.axis_index(axis))
    got = {}
    for k in offsets:
        if k in got:
            continue
        pairs = [(s, s - k) for s in range(count) if 0 <= s - k < count]
        if not pairs:
            got[k] = jnp.zeros_like(value)
            continue
        if -k in offsets and 2 * abs(k) >= count:
            pairs = pairs + [(s, s + k) for s in range(count) if 0 <= s + k < count]
            received = lax.ppermute(value, axis, pairs)
            for j in (k, -k):
                inside = jnp.logical_and(mine + j >= 0, mine + j < count)
                got[j] = jnp.where(inside, received, jnp.zeros_like(received))
            continue
        got[k] = lax.ppermute(value, axis, pairs)
    return got


def with_ring(cells, axis, dim, width, total):
    length = cells.shape[dim]
    head = lax.slice_in_dim(cells, 0, width, axis=dim)
    tail = lax.slice_in_dim(cells, length - width, length, axis=dim)
    if dim == cells.ndim - 1:
        def pack(values):
            return values.reshape(-1, width).T

        def unpack(values, shape):
            return values.T.reshape(shape)
    else:
        pack, unpack = (packed, unpacked)
    below = unpack(from_offsets(pack(tail), axis, (-1,))[-1], tail.shape)
    above = unpack(from_offsets(pack(head), axis, (1,))[1], head.shape)
    parts = [cells, above]
    gap = total - length - 2 * width
    if gap:
        gap_shape = list(cells.shape)
        gap_shape[dim] = gap
        parts.append(jnp.zeros(gap_shape, cells.dtype))
    parts.append(below)
    return jnp.concatenate(parts, axis=dim)


def ring_coordinates(start, length, width, total):
    marks = lax.broadcasted_iota(jnp.int32, (total,), 0)
    return jnp.where(
        marks < length + width,
        start + marks,
        jnp.where(marks >= total - width, start - (total - marks), -1),
    )


def packed(values):
    lanes = 128
    if values.size % lanes:
        return values.reshape(-1)
    return values.reshape(-1, lanes)


def unpacked(values, shape):
    return values.reshape(shape)


def upper_next(values, dimension):
    zeros_plane = jnp.zeros_like(lax.slice_in_dim(values, 0, 1, axis=dimension))
    rest = lax.slice_in_dim(values, 1, values.shape[dimension], axis=dimension)
    return jnp.concatenate([rest, zeros_plane], axis=dimension)


def lower_next(values, dimension):
    zeros_plane = jnp.zeros_like(lax.slice_in_dim(values, 0, 1, axis=dimension))
    rest = lax.slice_in_dim(values, 0, values.shape[dimension] - 1, axis=dimension)
    return jnp.concatenate([zeros_plane, rest], axis=dimension)


def forward_diff(values, dimension):
    return upper_next(values, dimension) - values


def backward_diff(values, dimension):
    return values - lower_next(values, dimension)


def curl_forward(field):
    field_x, field_y, field_z = field[0], field[1], field[2]
    return jnp.stack([forward_diff(field_z, 1) - forward_diff(field_y, 0),
                      forward_diff(field_x, 0) - forward_diff(field_z, 2),
                      forward_diff(field_y, 2) - forward_diff(field_x, 1)])


def curl_backward(field):
    field_x, field_y, field_z = field[0], field[1], field[2]
    return jnp.stack([backward_diff(field_z, 1) - backward_diff(field_y, 0),
                      backward_diff(field_x, 0) - backward_diff(field_z, 2),
                      backward_diff(field_y, 2) - backward_diff(field_x, 1)])


def advance_planes(values, amount, dimension):
    shape_pad = list(values.shape)
    shape_pad[dimension] = WSHIFT
    joined = jnp.concatenate([values, jnp.zeros(shape_pad, values.dtype)], axis=dimension)
    return lax.dynamic_slice_in_dim(joined, amount, values.shape[dimension], axis=dimension)


def cell_lookup(selector, table):
    return jnp.sum(jnp.where(selector, table[:, None, None], jnp.float32(0.0)), axis=0)


def inside_range(start, length, total, dimension, total_dims):
    shape_one = [1] * total_dims
    shape_one[dimension] = length
    marks = start + lax.broadcasted_iota(jnp.int32, tuple(shape_one), dimension)
    return jnp.logical_and(marks >= 0, marks < total)


def entering(value, axis):
    count, mine = (lax.axis_size(axis), lax.axis_index(axis))
    pieces = lax.all_gather(value, axis)
    running = jnp.zeros_like(value)
    for position in range(count - 1):
        running = jnp.where(position < mine, running + pieces[position], running)
    return running


def body(
    electric,
    magnetic,
    polarization,
    current,
    material,
    advance,
    permittivity,
    nonlinear,
    pole_strength,
    pole_frequency,
    pole_damping,
):
    planes, rows, columns = (electric.shape[1], electric.shape[2], electric.shape[3])
    n_prop, n_tx, n_ty = (lax.axis_size("prop"), lax.axis_size("tx"), lax.axis_size("ty"))
    total_z, total_y, total_x = (planes * n_prop, rows * n_ty, columns * n_tx)
    at_z, at_y, at_x = (lax.axis_index("prop"), lax.axis_index("ty"), lax.axis_index("tx"))
    halo = STEPS
    assert halo <= rows and halo <= columns

    state = jnp.concatenate(
        [
            electric,
            magnetic,
            polarization.reshape((-1,) + electric.shape[1:]),
            current.reshape((-1,) + electric.shape[1:]),
        ],
        axis=0,
    )

    below = -(-STEPS // planes)
    above = -(-(STEPS + STEPS * WSHIFT) // planes)
    whole_column = (below + above + 1) * planes >= total_z
    if whole_column:
        offsets = [k for k in range(-(n_prop - 1), n_prop) if k != 0]
        pieces = from_offsets(state, "prop", offsets)
        pieces[0] = state
        blocks = []
        for j in range(n_prop):
            block = jnp.zeros_like(state)
            for k, piece in pieces.items():
                block = jnp.where(at_z + k == j, piece, block)
            blocks.append(block)
        state = jnp.concatenate(blocks, axis=1)
        base_z = jnp.int32(0)
        own_z = at_z * planes
    else:
        offsets = [k for k in range(-below, above + 1) if k != 0]
        pieces = from_offsets(state, "prop", offsets)
        pieces[0] = state
        state = jnp.concatenate([pieces[k] for k in range(-below, above + 1)], axis=1)
        base_z = (at_z - below) * planes
        own_z = below * planes
    depth = state.shape[1]

    kinds = material.astype(jnp.float32)
    state = jnp.concatenate([state, jnp.broadcast_to(kinds[None, None], (1, depth, rows, columns))], axis=0)
    ring_rows = rows + 2 * halo
    tile = -(-2 * halo // 128) * 128
    ring_columns = columns + tile
    head = lax.slice_in_dim(state, 0, halo, axis=2)
    tail = lax.slice_in_dim(state, rows - halo, rows, axis=2)
    below = unpacked(from_offsets(packed(tail), "ty", (-1,))[-1], tail.shape)
    above = unpacked(from_offsets(packed(head), "ty", (1,))[1], head.shape)
    side = jnp.concatenate([above, below], axis=2)

    def columns_of(low, high):
        return jnp.concatenate(
            [lax.slice_in_dim(state, low, high, axis=3), lax.slice_in_dim(side, low, high, axis=3)], axis=2
        )

    x_head, x_tail = (columns_of(0, halo), columns_of(columns - halo, columns))
    strip_rows = -(-halo // 8) * 8
    strip_length = -(-x_head.size // halo // 128) * 128
    assert 2 * strip_rows <= tile

    def strip(values, at_top):
        flat = values.reshape(-1, halo).T
        room = strip_rows - halo
        rows_pad = (0, room) if at_top else (room, 0)
        return jnp.pad(flat, (rows_pad, (0, strip_length - flat.shape[1])))

    from_right = from_offsets(strip(x_head, True), "tx", (1,))[1]
    from_left = from_offsets(strip(x_tail, False), "tx", (-1,))[-1]

    place_z = base_z + lax.broadcasted_iota(jnp.int32, (depth,), 0)
    place_y = ring_coordinates(at_y * rows, rows, halo, ring_rows)
    place_x = ring_coordinates(at_x * columns, columns, halo, ring_columns)
    keep_mask = (
        ((place_z >= 0) & (place_z < total_z))[:, None, None]
        & ((place_y >= 0) & (place_y < total_y))[None, :, None]
        & ((place_x >= 0) & (place_x < total_x))[None, None, :]
    ).astype(jnp.float32)

    half_damp = 0.5 * time_step * pole_damping
    table = jnp.concatenate(
        [
            permittivity[None],
            nonlinear[None],
            pole_strength,
            (1.0 - half_damp) / (1.0 + half_damp),
            time_step * pole_frequency * pole_frequency / (1.0 + half_damp),
        ],
        axis=0,
    )

    own_at = jnp.reshape(jnp.asarray(own_z, jnp.int32), (1,))
    fields = state.shape[0]
    block = (planes, rows, columns)
    outs = pl.pallas_call(
        functools.partial(
            steps_kernel, planes=planes, rows=rows, columns=columns, whole=whole_column, total=total_z
        ),
        out_shape=(
            jax.ShapeDtypeStruct((3,) + block, jnp.float32),
            jax.ShapeDtypeStruct((3,) + block, jnp.float32),
            jax.ShapeDtypeStruct((2, 3) + block, jnp.float32),
            jax.ShapeDtypeStruct((2, 3) + block, jnp.float32),
            jax.ShapeDtypeStruct(block, jnp.float32),
        ),
        in_specs=[
            pl.BlockSpec(memory_space=pltpu.SMEM),
            pl.BlockSpec(memory_space=pltpu.SMEM),
            pl.BlockSpec(memory_space=pltpu.SMEM),
        ]
        + [pl.BlockSpec(memory_space=pltpu.VMEM) for _ in range(5)],
        out_specs=tuple(pl.BlockSpec(memory_space=pltpu.VMEM) for _ in range(5)),
        scratch_shapes=[
            pltpu.VMEM((fields, depth + WSHIFT, ring_rows, ring_columns), jnp.float32),
            pltpu.VMEM((depth, rows, columns), jnp.float32),
            pltpu.VMEM((tile, strip_length), jnp.float32),
            pltpu.VMEM((strip_length, tile), jnp.float32),
        ],
    )(advance, own_at, table, state, side, from_right, from_left, keep_mask)
    electric_o, magnetic_o, polarization_o, current_o, column_energy = outs
    if not whole_column:
        prefix = entering(jnp.sum(column_energy, axis=0), "prop")
        column_energy = (prefix[None] + jnp.cumsum(column_energy, axis=0)) / jnp.float32(total_z)
    return (electric_o, magnetic_o, polarization_o, current_o, column_energy)


def steps_kernel(
    advance_ref, own_ref, table_ref, state_ref, side_ref, right_ref, left_ref, mask_ref,
    electric_ref, magnetic_ref, polarization_ref, current_ref, energy_ref,
    work_ref, running_ref, strips_ref, turned_ref, *, planes, rows, columns, whole, total,
):
    fields, depth = (work_ref.shape[0], work_ref.shape[1] - WSHIFT)
    ring_rows = work_ref.shape[2]
    tile = strips_ref.shape[0]
    strip_rows = right_ref.shape[0]
    work_ref[:, depth:] = jnp.zeros((fields, WSHIFT) + work_ref.shape[2:], jnp.float32)
    strips_ref[...] = jnp.zeros(strips_ref.shape, jnp.float32)
    strips_ref[0:strip_rows] = right_ref[...]
    strips_ref[tile - strip_rows:tile] = left_ref[...]
    turned_ref[...] = strips_ref[...].T
    for c in range(fields):
        work_ref[c, 0:depth, 0:rows, 0:columns] = state_ref[c]
        work_ref[c, 0:depth, rows:, 0:columns] = side_ref[c]
        for z in range(depth):
            first_row = (c * depth + z) * ring_rows
            work_ref[c, z, :, columns:] = turned_ref[first_row:first_row + ring_rows]
    kinds = work_ref[fields - 1, 0]

    def lookup(row):
        cell = jnp.zeros(kinds.shape, jnp.float32)
        for m in range(table_ref.shape[1]):
            cell = jnp.where(kinds == jnp.float32(m), table_ref[row, m], cell)
        return cell

    eps_cell, kerr_cell = (lookup(0), lookup(1))
    strength, keep_rate, drive_rate = ((lookup(2), lookup(3)), (lookup(4), lookup(5)), (lookup(6), lookup(7)))
    keep_mask = mask_ref[...]
    zero_plane = jnp.zeros((1,) + keep_mask.shape[1:], jnp.float32)
    ring_rows, ring_columns = keep_mask.shape[1:]

    def up_z(f):
        return jnp.concatenate([f[1:], zero_plane], axis=0)

    def down_z(f):
        return jnp.concatenate([zero_plane, f[:-1]], axis=0)

    def up_y(f):
        return pltpu.roll(f, ring_rows - 1, 1)

    def down_y(f):
        return pltpu.roll(f, 1, 1)

    def up_x(f):
        return pltpu.roll(f, ring_columns - 1, 2)

    def down_x(f):
        return pltpu.roll(f, 1, 2)

    amount = 0
    for moment in range(STEPS):
        last = moment == STEPS - 1

        def own(f):
            return f[..., 0:rows, 0:columns] if last else f

        values = [work_ref[c, pl.ds(amount, depth)] for c in range(6)]
        if last:
            values += [work_ref[c, pl.ds(amount, depth), 0:rows, 0:columns] for c in range(6, fields - 1)]
        else:
            values += [work_ref[c, pl.ds(amount, depth)] for c in range(6, fields - 1)]
        e_x, e_y, e_z = values[0:3]
        h_x, h_y, h_z = values[3:6]
        pol = [values[6:9], values[9:12]]
        cur = [values[12:15], values[15:18]]
        h_x = (h_x - time_step * ((up_y(e_z) - e_z) - (up_z(e_y) - e_y))) * keep_mask
        h_y = (h_y - time_step * ((up_z(e_x) - e_x) - (up_x(e_z) - e_z))) * keep_mask
        h_z = (h_z - time_step * ((up_x(e_y) - e_y) - (up_y(e_x) - e_x))) * keep_mask
        electric = (own(e_x), own(e_y), own(e_z))
        squared = electric[0] * electric[0] + electric[1] * electric[1] + electric[2] * electric[2]
        for p in range(2):
            for c in range(3):
                cur[p][c] = own(keep_rate[p]) * cur[p][c] + own(drive_rate[p]) * (
                    own(strength[p]) * electric[c] - pol[p][c]
                )
                pol[p][c] = pol[p][c] + time_step * cur[p][c]
        curl_x = (own(h_z) - own(down_y(h_z))) - (own(h_y) - own(down_z(h_y)))
        curl_y = (own(h_x) - own(down_z(h_x))) - (own(h_z) - own(down_x(h_z)))
        curl_z = (own(h_y) - own(down_x(h_y))) - (own(h_x) - own(down_y(h_x)))
        denominator = own(eps_cell) + own(kerr_cell) * squared
        new_e = [
            (field + time_step * (curl - cur[0][c] - cur[1][c]) / denominator) * own(keep_mask)
            for c, (field, curl) in enumerate(zip(electric, (curl_x, curl_y, curl_z)))
        ]
        for c in range(3):
            work_ref[3 + c, 0:depth] = (h_x, h_y, h_z)[c]
        results = new_e + [None, None, None] + pol[0] + pol[1] + cur[0] + cur[1]
        for c in range(fields - 1):
            if c in (3, 4, 5):
                continue
            if last:
                work_ref[c, 0:depth, 0:rows, 0:columns] = results[c]
            else:
                work_ref[c, 0:depth] = results[c]
        amount = advance_ref[moment]

    start = amount + own_ref[0]
    for c in range(3):
        electric_ref[c] = work_ref[c, pl.ds(start, planes), 0:rows, 0:columns]
        magnetic_ref[c] = work_ref[3 + c, pl.ds(start, planes), 0:rows, 0:columns]
        for p in range(2):
            polarization_ref[p, c] = work_ref[6 + 3 * p + c, pl.ds(start, planes), 0:rows, 0:columns]
            current_ref[p, c] = work_ref[12 + 3 * p + c, pl.ds(start, planes), 0:rows, 0:columns]
    eps_own = eps_cell[0:rows, 0:columns]
    reach = depth if whole else planes
    first = amount if whole else start
    squared_e = None
    squared_h = None
    for c in range(3):
        e = work_ref[c, pl.ds(first, reach), 0:rows, 0:columns]
        h = work_ref[3 + c, pl.ds(first, reach), 0:rows, 0:columns]
        squared_e = e * e if squared_e is None else squared_e + e * e
        squared_h = h * h if squared_h is None else squared_h + h * h
    density = eps_own[None] * squared_e + squared_h
    if whole:
        total_so_far = density[0]
        running_ref[0] = total_so_far
        for z in range(1, depth):
            total_so_far = total_so_far + density[z]
            running_ref[z] = total_so_far
        energy_ref[...] = running_ref[pl.ds(own_ref[0], planes)] / jnp.float32(total)
    else:
        energy_ref[...] = density


def solution(mesh):
    return jax.shard_map(
        body,
        mesh=mesh,
        in_specs=(
            P(None, "prop", "ty", "tx"),
            P(None, "prop", "ty", "tx"),
            P(None, None, "prop", "ty", "tx"),
            P(None, None, "prop", "ty", "tx"),
            P("ty", "tx"),
            P(),
            P(),
            P(),
            P(),
            P(),
            P(),
        ),
        out_specs=(
            P(None, "prop", "ty", "tx"),
            P(None, "prop", "ty", "tx"),
            P(None, None, "prop", "ty", "tx"),
            P(None, None, "prop", "ty", "tx"),
            P("prop", "ty", "tx"),
        ),
        check_vma=False,
    )
```

```python
import functools

import jax
import jax.numpy as jnp
from jax import lax
from jax.experimental import pallas as pl
from jax.experimental.pallas import tpu as pltpu
from jax.sharding import PartitionSpec as P

STEPS = 4
WSHIFT = 2


time_step = 0.5


def from_offsets(value, axis, offsets):
    count, mine = (lax.axis_size(axis), lax.axis_index(axis))
    got = {}
    for k in offsets:
        if k in got:
            continue
        pairs = [(s, s - k) for s in range(count) if 0 <= s - k < count]
        if not pairs:
            got[k] = jnp.zeros_like(value)
            continue
        if -k in offsets and 2 * abs(k) >= count:
            pairs = pairs + [(s, s + k) for s in range(count) if 0 <= s + k < count]
            received = lax.ppermute(value, axis, pairs)
            for j in (k, -k):
                inside = jnp.logical_and(mine + j >= 0, mine + j < count)
                got[j] = jnp.where(inside, received, jnp.zeros_like(received))
            continue
        got[k] = lax.ppermute(value, axis, pairs)
    return got


def with_ring(cells, axis, dim, width, total):
    length = cells.shape[dim]
    head = lax.slice_in_dim(cells, 0, width, axis=dim)
    tail = lax.slice_in_dim(cells, length - width, length, axis=dim)
    if dim == cells.ndim - 1:
        def pack(values):
            return values.reshape(-1, width).T

        def unpack(values, shape):
            return values.T.reshape(shape)
    else:
        pack, unpack = (packed, unpacked)
    below = unpack(from_offsets(pack(tail), axis, (-1,))[-1], tail.shape)
    above = unpack(from_offsets(pack(head), axis, (1,))[1], head.shape)
    parts = [cells, above]
    gap = total - length - 2 * width
    if gap:
        gap_shape = list(cells.shape)
        gap_shape[dim] = gap
        parts.append(jnp.zeros(gap_shape, cells.dtype))
    parts.append(below)
    return jnp.concatenate(parts, axis=dim)


def ring_coordinates(start, length, width, total):
    marks = lax.broadcasted_iota(jnp.int32, (total,), 0)
    return jnp.where(
        marks < length + width,
        start + marks,
        jnp.where(marks >= total - width, start - (total - marks), -1),
    )


def packed(values):
    lanes = 128
    if values.size % lanes:
        return values.reshape(-1)
    return values.reshape(-1, lanes)


def unpacked(values, shape):
    return values.reshape(shape)


def upper_next(values, dimension):
    zeros_plane = jnp.zeros_like(lax.slice_in_dim(values, 0, 1, axis=dimension))
    rest = lax.slice_in_dim(values, 1, values.shape[dimension], axis=dimension)
    return jnp.concatenate([rest, zeros_plane], axis=dimension)


def lower_next(values, dimension):
    zeros_plane = jnp.zeros_like(lax.slice_in_dim(values, 0, 1, axis=dimension))
    rest = lax.slice_in_dim(values, 0, values.shape[dimension] - 1, axis=dimension)
    return jnp.concatenate([zeros_plane, rest], axis=dimension)


def forward_diff(values, dimension):
    return upper_next(values, dimension) - values


def backward_diff(values, dimension):
    return values - lower_next(values, dimension)


def curl_forward(field):
    field_x, field_y, field_z = field[0], field[1], field[2]
    return jnp.stack([forward_diff(field_z, 1) - forward_diff(field_y, 0),
                      forward_diff(field_x, 0) - forward_diff(field_z, 2),
                      forward_diff(field_y, 2) - forward_diff(field_x, 1)])


def curl_backward(field):
    field_x, field_y, field_z = field[0], field[1], field[2]
    return jnp.stack([backward_diff(field_z, 1) - backward_diff(field_y, 0),
                      backward_diff(field_x, 0) - backward_diff(field_z, 2),
                      backward_diff(field_y, 2) - backward_diff(field_x, 1)])


def advance_planes(values, amount, dimension):
    shape_pad = list(values.shape)
    shape_pad[dimension] = WSHIFT
    joined = jnp.concatenate([values, jnp.zeros(shape_pad, values.dtype)], axis=dimension)
    return lax.dynamic_slice_in_dim(joined, amount, values.shape[dimension], axis=dimension)


def cell_lookup(selector, table):
    return jnp.sum(jnp.where(selector, table[:, None, None], jnp.float32(0.0)), axis=0)


def inside_range(start, length, total, dimension, total_dims):
    shape_one = [1] * total_dims
    shape_one[dimension] = length
    marks = start + lax.broadcasted_iota(jnp.int32, tuple(shape_one), dimension)
    return jnp.logical_and(marks >= 0, marks < total)


def entering(value, axis):
    count, mine = (lax.axis_size(axis), lax.axis_index(axis))
    pieces = lax.all_gather(value, axis)
    running = jnp.zeros_like(value)
    for position in range(count - 1):
        running = jnp.where(position < mine, running + pieces[position], running)
    return running


def body(
    electric,
    magnetic,
    polarization,
    current,
    material,
    advance,
    permittivity,
    nonlinear,
    pole_strength,
    pole_frequency,
    pole_damping,
):
    planes, rows, columns = (electric.shape[1], electric.shape[2], electric.shape[3])
    n_prop, n_tx, n_ty = (lax.axis_size("prop"), lax.axis_size("tx"), lax.axis_size("ty"))
    total_z, total_y, total_x = (planes * n_prop, rows * n_ty, columns * n_tx)
    at_z, at_y, at_x = (lax.axis_index("prop"), lax.axis_index("ty"), lax.axis_index("tx"))
    halo = STEPS
    assert halo <= rows and halo <= columns

    state = jnp.concatenate(
        [
            electric,
            magnetic,
            polarization.reshape((-1,) + electric.shape[1:]),
            current.reshape((-1,) + electric.shape[1:]),
        ],
        axis=0,
    )

    below = -(-STEPS // planes)
    above = -(-(STEPS + STEPS * WSHIFT) // planes)
    whole_column = (below + above + 1) * planes >= total_z
    if whole_column and n_prop == 2:
        partner = lax.ppermute(state, "prop", [(0, 1), (1, 0)])
        kernel_blocks = [state, partner]
        block_at = jnp.stack([at_z * planes, (1 - at_z) * planes]).astype(jnp.int32)
        state = jnp.concatenate(kernel_blocks, axis=1)
        base_z = jnp.int32(0)
        own_z = at_z * planes
    elif whole_column:
        offsets = [k for k in range(-(n_prop - 1), n_prop) if k != 0]
        pieces = from_offsets(state, "prop", offsets)
        pieces[0] = state
        blocks = []
        for j in range(n_prop):
            block = jnp.zeros_like(state)
            for k, piece in pieces.items():
                block = jnp.where(at_z + k == j, piece, block)
            blocks.append(block)
        state = jnp.concatenate(blocks, axis=1)
        base_z = jnp.int32(0)
        own_z = at_z * planes
    else:
        offsets = [k for k in range(-below, above + 1) if k != 0]
        pieces = from_offsets(state, "prop", offsets)
        pieces[0] = state
        state = jnp.concatenate([pieces[k] for k in range(-below, above + 1)], axis=1)
        base_z = (at_z - below) * planes
        own_z = below * planes
    if not (whole_column and n_prop == 2):
        kernel_blocks = [state]
        block_at = jnp.zeros((1,), jnp.int32)
    depth = state.shape[1]

    kinds = material.astype(jnp.float32)
    kinds_own = kinds
    state = jnp.concatenate([state, jnp.broadcast_to(kinds[None, None], (1, depth, rows, columns))], axis=0)
    ring_rows = rows + 2 * halo
    tile = -(-2 * halo // 128) * 128
    ring_columns = columns + tile
    head = lax.slice_in_dim(state, 0, halo, axis=2)
    tail = lax.slice_in_dim(state, rows - halo, rows, axis=2)
    below = unpacked(from_offsets(packed(tail), "ty", (-1,))[-1], tail.shape)
    above = unpacked(from_offsets(packed(head), "ty", (1,))[1], head.shape)
    side = jnp.concatenate([above, below], axis=2)

    def columns_of(low, high):
        return jnp.concatenate(
            [lax.slice_in_dim(state, low, high, axis=3), lax.slice_in_dim(side, low, high, axis=3)], axis=2
        )

    x_head, x_tail = (columns_of(0, halo), columns_of(columns - halo, columns))
    strip_rows = -(-halo // 8) * 8
    strip_length = -(-x_head.size // halo // 128) * 128
    assert 2 * strip_rows <= tile

    def strip(values, at_top):
        flat = values.reshape(-1, halo).T
        room = strip_rows - halo
        rows_pad = (0, room) if at_top else (room, 0)
        return jnp.pad(flat, (rows_pad, (0, strip_length - flat.shape[1])))

    from_right = from_offsets(strip(x_head, True), "tx", (1,))[1]
    from_left = from_offsets(strip(x_tail, False), "tx", (-1,))[-1]

    place_z = base_z + lax.broadcasted_iota(jnp.int32, (depth,), 0)
    place_y = ring_coordinates(at_y * rows, rows, halo, ring_rows)
    place_x = ring_coordinates(at_x * columns, columns, halo, ring_columns)
    keep_mask = (
        ((place_z >= 0) & (place_z < total_z))[:, None, None]
        & ((place_y >= 0) & (place_y < total_y))[None, :, None]
        & ((place_x >= 0) & (place_x < total_x))[None, None, :]
    ).astype(jnp.float32)

    half_damp = 0.5 * time_step * pole_damping
    table = jnp.concatenate(
        [
            permittivity[None],
            nonlinear[None],
            pole_strength,
            (1.0 - half_damp) / (1.0 + half_damp),
            time_step * pole_frequency * pole_frequency / (1.0 + half_damp),
        ],
        axis=0,
    )

    own_at = jnp.reshape(jnp.asarray(own_z, jnp.int32), (1,))
    fields = state.shape[0]
    block = (planes, rows, columns)
    outs = pl.pallas_call(
        functools.partial(
            steps_kernel, planes=planes, rows=rows, columns=columns, whole=whole_column, total=total_z,
            blocks=len(kernel_blocks),
        ),
        out_shape=(
            jax.ShapeDtypeStruct((3,) + block, jnp.float32),
            jax.ShapeDtypeStruct((3,) + block, jnp.float32),
            jax.ShapeDtypeStruct((2, 3) + block, jnp.float32),
            jax.ShapeDtypeStruct((2, 3) + block, jnp.float32),
            jax.ShapeDtypeStruct(block, jnp.float32),
        ),
        in_specs=[
            pl.BlockSpec(memory_space=pltpu.SMEM),
            pl.BlockSpec(memory_space=pltpu.SMEM),
            pl.BlockSpec(memory_space=pltpu.SMEM),
            pl.BlockSpec(memory_space=pltpu.SMEM),
        ]
        + [pl.BlockSpec(memory_space=pltpu.VMEM) for _ in range(len(kernel_blocks) + 5)],
        out_specs=tuple(pl.BlockSpec(memory_space=pltpu.VMEM) for _ in range(5)),
        scratch_shapes=[
            pltpu.VMEM((fields, depth + WSHIFT, ring_rows, ring_columns), jnp.float32),
            pltpu.VMEM((depth, rows, columns), jnp.float32),
            pltpu.VMEM((tile, strip_length), jnp.float32),
            pltpu.VMEM((strip_length, tile), jnp.float32),
        ],
    )(advance, own_at, block_at, table, kinds_own, *kernel_blocks, side, from_right, from_left, keep_mask)
    electric_o, magnetic_o, polarization_o, current_o, column_energy = outs
    if not whole_column:
        prefix = entering(jnp.sum(column_energy, axis=0), "prop")
        column_energy = (prefix[None] + jnp.cumsum(column_energy, axis=0)) / jnp.float32(total_z)
    return (electric_o, magnetic_o, polarization_o, current_o, column_energy)


def steps_kernel(
    advance_ref, own_ref, block_at_ref, table_ref, kinds_ref, *refs, planes, rows, columns, whole, total, blocks,
):
    block_refs = refs[:blocks]
    (side_ref, right_ref, left_ref, mask_ref,
     electric_ref, magnetic_ref, polarization_ref, current_ref, energy_ref,
     work_ref, running_ref, strips_ref, turned_ref) = refs[blocks:]
    fields, depth = (work_ref.shape[0], work_ref.shape[1] - WSHIFT)
    ring_rows = work_ref.shape[2]
    tile = strips_ref.shape[0]
    strip_rows = right_ref.shape[0]
    work_ref[:, depth:] = jnp.zeros((fields, WSHIFT) + work_ref.shape[2:], jnp.float32)
    strips_ref[...] = jnp.zeros(strips_ref.shape, jnp.float32)
    strips_ref[0:strip_rows] = right_ref[...]
    strips_ref[tile - strip_rows:tile] = left_ref[...]
    turned_ref[...] = strips_ref[...].T
    work_ref[fields - 1, 0, 0:rows, 0:columns] = kinds_ref[...]
    local = 0
    for b, block_ref in enumerate(block_refs):
        size = block_ref.shape[1]
        at = block_at_ref[b]
        for c in range(fields):
            if c < fields - 1:
                work_ref[c, pl.ds(at, size), 0:rows, 0:columns] = block_ref[c]
            work_ref[c, pl.ds(at, size), rows:, 0:columns] = side_ref[c, local:local + size]
            for z in range(size):
                first_row = (c * depth + local + z) * ring_rows
                work_ref[c, at + z, :, columns:] = turned_ref[first_row:first_row + ring_rows]
        local += size
    kinds = work_ref[fields - 1, 0]

    def lookup(row):
        cell = jnp.zeros(kinds.shape, jnp.float32)
        for m in range(table_ref.shape[1]):
            cell = jnp.where(kinds == jnp.float32(m), table_ref[row, m], cell)
        return cell

    eps_cell, kerr_cell = (lookup(0), lookup(1))
    strength, keep_rate, drive_rate = ((lookup(2), lookup(3)), (lookup(4), lookup(5)), (lookup(6), lookup(7)))
    keep_mask = mask_ref[...]
    zero_plane = jnp.zeros((1,) + keep_mask.shape[1:], jnp.float32)
    ring_rows, ring_columns = keep_mask.shape[1:]

    def up_z(f):
        return jnp.concatenate([f[1:], zero_plane], axis=0)

    def down_z(f):
        return jnp.concatenate([zero_plane, f[:-1]], axis=0)

    def up_y(f):
        return pltpu.roll(f, ring_rows - 1, 1)

    def down_y(f):
        return pltpu.roll(f, 1, 1)

    def up_x(f):
        return pltpu.roll(f, ring_columns - 1, 2)

    def down_x(f):
        return pltpu.roll(f, 1, 2)

    amount = 0
    for moment in range(STEPS):
        last = moment == STEPS - 1

        def own(f):
            return f[..., 0:rows, 0:columns] if last else f

        values = [work_ref[c, pl.ds(amount, depth)] for c in range(6)]
        if last:
            values += [work_ref[c, pl.ds(amount, depth), 0:rows, 0:columns] for c in range(6, fields - 1)]
        else:
            values += [work_ref[c, pl.ds(amount, depth)] for c in range(6, fields - 1)]
        e_x, e_y, e_z = values[0:3]
        h_x, h_y, h_z = values[3:6]
        pol = [values[6:9], values[9:12]]
        cur = [values[12:15], values[15:18]]
        h_x = (h_x - time_step * ((up_y(e_z) - e_z) - (up_z(e_y) - e_y))) * keep_mask
        h_y = (h_y - time_step * ((up_z(e_x) - e_x) - (up_x(e_z) - e_z))) * keep_mask
        h_z = (h_z - time_step * ((up_x(e_y) - e_y) - (up_y(e_x) - e_x))) * keep_mask
        electric = (own(e_x), own(e_y), own(e_z))
        squared = electric[0] * electric[0] + electric[1] * electric[1] + electric[2] * electric[2]
        for p in range(2):
            for c in range(3):
                cur[p][c] = own(keep_rate[p]) * cur[p][c] + own(drive_rate[p]) * (
                    own(strength[p]) * electric[c] - pol[p][c]
                )
                pol[p][c] = pol[p][c] + time_step * cur[p][c]
        curl_x = (own(h_z) - own(down_y(h_z))) - (own(h_y) - own(down_z(h_y)))
        curl_y = (own(h_x) - own(down_z(h_x))) - (own(h_z) - own(down_x(h_z)))
        curl_z = (own(h_y) - own(down_x(h_y))) - (own(h_x) - own(down_y(h_x)))
        denominator = own(eps_cell) + own(kerr_cell) * squared
        new_e = [
            (field + time_step * (curl - cur[0][c] - cur[1][c]) / denominator) * own(keep_mask)
            for c, (field, curl) in enumerate(zip(electric, (curl_x, curl_y, curl_z)))
        ]
        for c in range(3):
            work_ref[3 + c, 0:depth] = (h_x, h_y, h_z)[c]
        results = new_e + [None, None, None] + pol[0] + pol[1] + cur[0] + cur[1]
        for c in range(fields - 1):
            if c in (3, 4, 5):
                continue
            if last:
                work_ref[c, 0:depth, 0:rows, 0:columns] = results[c]
            else:
                work_ref[c, 0:depth] = results[c]
        amount = advance_ref[moment]

    start = amount + own_ref[0]
    for c in range(3):
        electric_ref[c] = work_ref[c, pl.ds(start, planes), 0:rows, 0:columns]
        magnetic_ref[c] = work_ref[3 + c, pl.ds(start, planes), 0:rows, 0:columns]
        for p in range(2):
            polarization_ref[p, c] = work_ref[6 + 3 * p + c, pl.ds(start, planes), 0:rows, 0:columns]
            current_ref[p, c] = work_ref[12 + 3 * p + c, pl.ds(start, planes), 0:rows, 0:columns]
    eps_own = eps_cell[0:rows, 0:columns]
    reach = depth if whole else planes
    first = amount if whole else start
    squared_e = None
    squared_h = None
    for c in range(3):
        e = work_ref[c, pl.ds(first, reach), 0:rows, 0:columns]
        h = work_ref[3 + c, pl.ds(first, reach), 0:rows, 0:columns]
        squared_e = e * e if squared_e is None else squared_e + e * e
        squared_h = h * h if squared_h is None else squared_h + h * h
    density = eps_own[None] * squared_e + squared_h
    if whole:
        total_so_far = density[0]
        running_ref[0] = total_so_far
        for z in range(1, depth):
            total_so_far = total_so_far + density[z]
            running_ref[z] = total_so_far
        energy_ref[...] = running_ref[pl.ds(own_ref[0], planes)] / jnp.float32(total)
    else:
        energy_ref[...] = density


def solution(mesh):
    return jax.shard_map(
        body,
        mesh=mesh,
        in_specs=(
            P(None, "prop", "ty", "tx"),
            P(None, "prop", "ty", "tx"),
            P(None, None, "prop", "ty", "tx"),
            P(None, None, "prop", "ty", "tx"),
            P("ty", "tx"),
            P(),
            P(),
            P(),
            P(),
            P(),
            P(),
        ),
        out_specs=(
            P(None, "prop", "ty", "tx"),
            P(None, "prop", "ty", "tx"),
            P(None, None, "prop", "ty", "tx"),
            P(None, None, "prop", "ty", "tx"),
            P("prop", "ty", "tx"),
        ),
        check_vma=False,
    )
```

```python
import functools

import jax
import jax.numpy as jnp
from jax import lax
from jax.experimental import pallas as pl
from jax.experimental.pallas import tpu as pltpu
from jax.sharding import PartitionSpec as P

STEPS = 4
WSHIFT = 2


time_step = 0.5


def from_offsets(value, axis, offsets):
    count, mine = (lax.axis_size(axis), lax.axis_index(axis))
    got = {}
    for k in offsets:
        if k in got:
            continue
        pairs = [(s, s - k) for s in range(count) if 0 <= s - k < count]
        if not pairs:
            got[k] = jnp.zeros_like(value)
            continue
        if -k in offsets and 2 * abs(k) >= count:
            pairs = pairs + [(s, s + k) for s in range(count) if 0 <= s + k < count]
            received = lax.ppermute(value, axis, pairs)
            for j in (k, -k):
                inside = jnp.logical_and(mine + j >= 0, mine + j < count)
                got[j] = jnp.where(inside, received, jnp.zeros_like(received))
            continue
        got[k] = lax.ppermute(value, axis, pairs)
    return got


def with_ring(cells, axis, dim, width, total):
    length = cells.shape[dim]
    head = lax.slice_in_dim(cells, 0, width, axis=dim)
    tail = lax.slice_in_dim(cells, length - width, length, axis=dim)
    if dim == cells.ndim - 1:
        def pack(values):
            return values.reshape(-1, width).T

        def unpack(values, shape):
            return values.T.reshape(shape)
    else:
        pack, unpack = (packed, unpacked)
    below = unpack(from_offsets(pack(tail), axis, (-1,))[-1], tail.shape)
    above = unpack(from_offsets(pack(head), axis, (1,))[1], head.shape)
    parts = [cells, above]
    gap = total - length - 2 * width
    if gap:
        gap_shape = list(cells.shape)
        gap_shape[dim] = gap
        parts.append(jnp.zeros(gap_shape, cells.dtype))
    parts.append(below)
    return jnp.concatenate(parts, axis=dim)


def ring_coordinates(start, length, width, total):
    marks = lax.broadcasted_iota(jnp.int32, (total,), 0)
    return jnp.where(
        marks < length + width,
        start + marks,
        jnp.where(marks >= total - width, start - (total - marks), -1),
    )


def packed(values):
    lanes = 128
    if values.size % lanes:
        return values.reshape(-1)
    return values.reshape(-1, lanes)


def unpacked(values, shape):
    return values.reshape(shape)


def upper_next(values, dimension):
    zeros_plane = jnp.zeros_like(lax.slice_in_dim(values, 0, 1, axis=dimension))
    rest = lax.slice_in_dim(values, 1, values.shape[dimension], axis=dimension)
    return jnp.concatenate([rest, zeros_plane], axis=dimension)


def lower_next(values, dimension):
    zeros_plane = jnp.zeros_like(lax.slice_in_dim(values, 0, 1, axis=dimension))
    rest = lax.slice_in_dim(values, 0, values.shape[dimension] - 1, axis=dimension)
    return jnp.concatenate([zeros_plane, rest], axis=dimension)


def forward_diff(values, dimension):
    return upper_next(values, dimension) - values


def backward_diff(values, dimension):
    return values - lower_next(values, dimension)


def curl_forward(field):
    field_x, field_y, field_z = field[0], field[1], field[2]
    return jnp.stack([forward_diff(field_z, 1) - forward_diff(field_y, 0),
                      forward_diff(field_x, 0) - forward_diff(field_z, 2),
                      forward_diff(field_y, 2) - forward_diff(field_x, 1)])


def curl_backward(field):
    field_x, field_y, field_z = field[0], field[1], field[2]
    return jnp.stack([backward_diff(field_z, 1) - backward_diff(field_y, 0),
                      backward_diff(field_x, 0) - backward_diff(field_z, 2),
                      backward_diff(field_y, 2) - backward_diff(field_x, 1)])


def advance_planes(values, amount, dimension):
    shape_pad = list(values.shape)
    shape_pad[dimension] = WSHIFT
    joined = jnp.concatenate([values, jnp.zeros(shape_pad, values.dtype)], axis=dimension)
    return lax.dynamic_slice_in_dim(joined, amount, values.shape[dimension], axis=dimension)


def cell_lookup(selector, table):
    return jnp.sum(jnp.where(selector, table[:, None, None], jnp.float32(0.0)), axis=0)


def inside_range(start, length, total, dimension, total_dims):
    shape_one = [1] * total_dims
    shape_one[dimension] = length
    marks = start + lax.broadcasted_iota(jnp.int32, tuple(shape_one), dimension)
    return jnp.logical_and(marks >= 0, marks < total)


def entering(value, axis):
    count, mine = (lax.axis_size(axis), lax.axis_index(axis))
    pieces = lax.all_gather(value, axis)
    running = jnp.zeros_like(value)
    for position in range(count - 1):
        running = jnp.where(position < mine, running + pieces[position], running)
    return running


def body(
    electric,
    magnetic,
    polarization,
    current,
    material,
    advance,
    permittivity,
    nonlinear,
    pole_strength,
    pole_frequency,
    pole_damping,
):
    planes, rows, columns = (electric.shape[1], electric.shape[2], electric.shape[3])
    n_prop, n_tx, n_ty = (lax.axis_size("prop"), lax.axis_size("tx"), lax.axis_size("ty"))
    total_z, total_y, total_x = (planes * n_prop, rows * n_ty, columns * n_tx)
    at_z, at_y, at_x = (lax.axis_index("prop"), lax.axis_index("ty"), lax.axis_index("tx"))
    halo = STEPS
    assert halo <= rows and halo <= columns

    state = jnp.concatenate(
        [
            electric,
            magnetic,
            polarization.reshape((-1,) + electric.shape[1:]),
            current.reshape((-1,) + electric.shape[1:]),
        ],
        axis=0,
    )

    below = -(-STEPS // planes)
    above = -(-(STEPS + STEPS * WSHIFT) // planes)
    whole_column = (below + above + 1) * planes >= total_z
    if whole_column:
        offsets = [k for k in range(-(n_prop - 1), n_prop) if k != 0]
        pieces = from_offsets(state, "prop", offsets)
        pieces[0] = state
        blocks = []
        for j in range(n_prop):
            block = jnp.zeros_like(state)
            for k, piece in pieces.items():
                block = jnp.where(at_z + k == j, piece, block)
            blocks.append(block)
        state = jnp.concatenate(blocks, axis=1)
        base_z = jnp.int32(0)
        own_z = at_z * planes
    else:
        offsets = [k for k in range(-below, above + 1) if k != 0]
        pieces = from_offsets(state, "prop", offsets)
        pieces[0] = state
        state = jnp.concatenate([pieces[k] for k in range(-below, above + 1)], axis=1)
        base_z = (at_z - below) * planes
        own_z = below * planes
    depth = state.shape[1]

    kinds = material.astype(jnp.float32)
    state = jnp.concatenate([state, jnp.broadcast_to(kinds[None, None], (1, depth, rows, columns))], axis=0)
    ring_rows = rows + 2 * halo
    tile = -(-2 * halo // 128) * 128
    ring_columns = columns + tile
    head = lax.slice_in_dim(state, 0, halo, axis=2)
    tail = lax.slice_in_dim(state, rows - halo, rows, axis=2)
    below = unpacked(from_offsets(packed(tail), "ty", (-1,))[-1], tail.shape)
    above = unpacked(from_offsets(packed(head), "ty", (1,))[1], head.shape)
    side = jnp.concatenate([above, below], axis=2)

    def columns_of(low, high):
        return jnp.concatenate(
            [lax.slice_in_dim(state, low, high, axis=3), lax.slice_in_dim(side, low, high, axis=3)], axis=2
        )

    x_head, x_tail = (columns_of(0, halo), columns_of(columns - halo, columns))
    strip_rows = -(-halo // 8) * 8
    strip_length = -(-x_head.size // halo // 128) * 128
    assert 2 * strip_rows <= tile

    def strip(values, at_top):
        flat = values.reshape(-1, halo).T
        room = strip_rows - halo
        rows_pad = (0, room) if at_top else (room, 0)
        return jnp.pad(flat, (rows_pad, (0, strip_length - flat.shape[1])))

    from_right = from_offsets(strip(x_head, True), "tx", (1,))[1]
    from_left = from_offsets(strip(x_tail, False), "tx", (-1,))[-1]

    place_z = base_z + lax.broadcasted_iota(jnp.int32, (depth,), 0)
    place_y = ring_coordinates(at_y * rows, rows, halo, ring_rows)
    place_x = ring_coordinates(at_x * columns, columns, halo, ring_columns)
    keep_mask = (
        ((place_z >= 0) & (place_z < total_z))[:, None, None]
        & ((place_y >= 0) & (place_y < total_y))[None, :, None]
        & ((place_x >= 0) & (place_x < total_x))[None, None, :]
    ).astype(jnp.float32)

    half_damp = 0.5 * time_step * pole_damping
    table = jnp.concatenate(
        [
            permittivity[None],
            nonlinear[None],
            pole_strength,
            (1.0 - half_damp) / (1.0 + half_damp),
            time_step * pole_frequency * pole_frequency / (1.0 + half_damp),
        ],
        axis=0,
    )

    own_at = jnp.reshape(jnp.asarray(own_z, jnp.int32), (1,))
    fields = state.shape[0]
    block = (planes, rows, columns)
    outs = pl.pallas_call(
        functools.partial(
            steps_kernel, planes=planes, rows=rows, columns=columns, whole=whole_column, total=total_z
        ),
        out_shape=(
            jax.ShapeDtypeStruct((3,) + block, jnp.float32),
            jax.ShapeDtypeStruct((3,) + block, jnp.float32),
            jax.ShapeDtypeStruct((2, 3) + block, jnp.float32),
            jax.ShapeDtypeStruct((2, 3) + block, jnp.float32),
            jax.ShapeDtypeStruct(block, jnp.float32),
        ),
        in_specs=[
            pl.BlockSpec(memory_space=pltpu.SMEM),
            pl.BlockSpec(memory_space=pltpu.SMEM),
            pl.BlockSpec(memory_space=pltpu.SMEM),
        ]
        + [pl.BlockSpec(memory_space=pltpu.VMEM) for _ in range(5)],
        out_specs=tuple(pl.BlockSpec(memory_space=pltpu.VMEM) for _ in range(5)),
        scratch_shapes=[
            pltpu.VMEM((fields, depth + WSHIFT, ring_rows, ring_columns), jnp.float32),
            pltpu.VMEM((depth, rows, columns), jnp.float32),
            pltpu.VMEM((tile, strip_length), jnp.float32),
            pltpu.VMEM((strip_length, tile), jnp.float32),
        ],
    )(advance, own_at, table, state, side, from_right, from_left, keep_mask)
    electric_o, magnetic_o, polarization_o, current_o, column_energy = outs
    if not whole_column:
        prefix = entering(jnp.sum(column_energy, axis=0), "prop")
        column_energy = (prefix[None] + jnp.cumsum(column_energy, axis=0)) / jnp.float32(total_z)
    return (electric_o, magnetic_o, polarization_o, current_o, column_energy)


def steps_kernel(
    advance_ref, own_ref, table_ref, state_ref, side_ref, right_ref, left_ref, mask_ref,
    electric_ref, magnetic_ref, polarization_ref, current_ref, energy_ref,
    work_ref, running_ref, strips_ref, turned_ref, *, planes, rows, columns, whole, total,
):
    fields, depth = (work_ref.shape[0], work_ref.shape[1] - WSHIFT)
    ring_rows = work_ref.shape[2]
    tile = strips_ref.shape[0]
    strip_rows = right_ref.shape[0]
    work_ref[0:fields - 1, depth:] = jnp.zeros((fields - 1, WSHIFT) + work_ref.shape[2:], jnp.float32)
    strips_ref[strip_rows:tile - strip_rows] = jnp.zeros((tile - 2 * strip_rows, strips_ref.shape[1]), jnp.float32)
    strips_ref[0:strip_rows] = right_ref[...]
    strips_ref[tile - strip_rows:tile] = left_ref[...]
    turned_ref[...] = strips_ref[...].T
    for c in range(fields):
        work_ref[c, 0:depth, 0:rows, 0:columns] = state_ref[c]
        work_ref[c, 0:depth, rows:, 0:columns] = side_ref[c]
        for z in range(depth):
            first_row = (c * depth + z) * ring_rows
            work_ref[c, z, :, columns:] = turned_ref[first_row:first_row + ring_rows]
    kinds = work_ref[fields - 1, 0]

    def lookup(row):
        cell = jnp.zeros(kinds.shape, jnp.float32)
        for m in range(table_ref.shape[1]):
            cell = jnp.where(kinds == jnp.float32(m), table_ref[row, m], cell)
        return cell

    eps_cell, kerr_cell = (lookup(0), lookup(1))
    strength, keep_rate, drive_rate = ((lookup(2), lookup(3)), (lookup(4), lookup(5)), (lookup(6), lookup(7)))
    keep_mask = mask_ref[...]
    zero_plane = jnp.zeros((1,) + keep_mask.shape[1:], jnp.float32)
    ring_rows, ring_columns = keep_mask.shape[1:]

    def up_z(f):
        return jnp.concatenate([f[1:], zero_plane], axis=0)

    def down_z(f):
        return jnp.concatenate([zero_plane, f[:-1]], axis=0)

    def up_y(f):
        return pltpu.roll(f, ring_rows - 1, 1)

    def down_y(f):
        return pltpu.roll(f, 1, 1)

    def up_x(f):
        return pltpu.roll(f, ring_columns - 1, 2)

    def down_x(f):
        return pltpu.roll(f, 1, 2)

    amount = 0
    for moment in range(STEPS):
        last = moment == STEPS - 1

        def own(f):
            return f[..., 0:rows, 0:columns] if last else f

        values = [work_ref[c, pl.ds(amount, depth)] for c in range(6)]
        if last:
            values += [work_ref[c, pl.ds(amount, depth), 0:rows, 0:columns] for c in range(6, fields - 1)]
        else:
            values += [work_ref[c, pl.ds(amount, depth)] for c in range(6, fields - 1)]
        e_x, e_y, e_z = values[0:3]
        h_x, h_y, h_z = values[3:6]
        pol = [values[6:9], values[9:12]]
        cur = [values[12:15], values[15:18]]
        h_x = (h_x - time_step * ((up_y(e_z) - e_z) - (up_z(e_y) - e_y))) * keep_mask
        h_y = (h_y - time_step * ((up_z(e_x) - e_x) - (up_x(e_z) - e_z))) * keep_mask
        h_z = (h_z - time_step * ((up_x(e_y) - e_y) - (up_y(e_x) - e_x))) * keep_mask
        electric = (own(e_x), own(e_y), own(e_z))
        squared = electric[0] * electric[0] + electric[1] * electric[1] + electric[2] * electric[2]
        for p in range(2):
            for c in range(3):
                cur[p][c] = own(keep_rate[p]) * cur[p][c] + own(drive_rate[p]) * (
                    own(strength[p]) * electric[c] - pol[p][c]
                )
                pol[p][c] = pol[p][c] + time_step * cur[p][c]
        curl_x = (own(h_z) - own(down_y(h_z))) - (own(h_y) - own(down_z(h_y)))
        curl_y = (own(h_x) - own(down_z(h_x))) - (own(h_z) - own(down_x(h_z)))
        curl_z = (own(h_y) - own(down_x(h_y))) - (own(h_x) - own(down_y(h_x)))
        denominator = own(eps_cell) + own(kerr_cell) * squared
        new_e = [
            (field + time_step * (curl - cur[0][c] - cur[1][c]) / denominator) * own(keep_mask)
            for c, (field, curl) in enumerate(zip(electric, (curl_x, curl_y, curl_z)))
        ]
        for c in range(3):
            work_ref[3 + c, 0:depth] = (h_x, h_y, h_z)[c]
        results = new_e + [None, None, None] + pol[0] + pol[1] + cur[0] + cur[1]
        for c in range(fields - 1):
            if c in (3, 4, 5):
                continue
            if last:
                work_ref[c, 0:depth, 0:rows, 0:columns] = results[c]
            else:
                work_ref[c, 0:depth] = results[c]
        amount = advance_ref[moment]

    start = amount + own_ref[0]
    for c in range(3):
        electric_ref[c] = work_ref[c, pl.ds(start, planes), 0:rows, 0:columns]
        magnetic_ref[c] = work_ref[3 + c, pl.ds(start, planes), 0:rows, 0:columns]
        for p in range(2):
            polarization_ref[p, c] = work_ref[6 + 3 * p + c, pl.ds(start, planes), 0:rows, 0:columns]
            current_ref[p, c] = work_ref[12 + 3 * p + c, pl.ds(start, planes), 0:rows, 0:columns]
    eps_own = eps_cell[0:rows, 0:columns]
    reach = depth if whole else planes
    first = amount if whole else start
    squared_e = None
    squared_h = None
    for c in range(3):
        e = work_ref[c, pl.ds(first, reach), 0:rows, 0:columns]
        h = work_ref[3 + c, pl.ds(first, reach), 0:rows, 0:columns]
        squared_e = e * e if squared_e is None else squared_e + e * e
        squared_h = h * h if squared_h is None else squared_h + h * h
    density = eps_own[None] * squared_e + squared_h
    if whole:
        total_so_far = density[0]
        running_ref[0] = total_so_far
        for z in range(1, depth):
            total_so_far = total_so_far + density[z]
            running_ref[z] = total_so_far
        energy_ref[...] = running_ref[pl.ds(own_ref[0], planes)] / jnp.float32(total)
    else:
        energy_ref[...] = density


def solution(mesh):
    return jax.shard_map(
        body,
        mesh=mesh,
        in_specs=(
            P(None, "prop", "ty", "tx"),
            P(None, "prop", "ty", "tx"),
            P(None, None, "prop", "ty", "tx"),
            P(None, None, "prop", "ty", "tx"),
            P("ty", "tx"),
            P(),
            P(),
            P(),
            P(),
            P(),
            P(),
        ),
        out_specs=(
            P(None, "prop", "ty", "tx"),
            P(None, "prop", "ty", "tx"),
            P(None, None, "prop", "ty", "tx"),
            P(None, None, "prop", "ty", "tx"),
            P("prop", "ty", "tx"),
        ),
        check_vma=False,
    )
```
